256 devices in a mesh: dp: 4 (over y), head: 4 (over x), seq: 16 (over z, core).
Axes of the slice: x: 4, y: 4, z: 8, core: 2. Of those that a mesh axis runs over, the one named last changes fastest.
Arguments:
- q_dense: bfloat16 [32768, 8, 128], P(('dp', 'seq'), 'head'), parts along dimension 0, may hold values from -108 to 108
- k_dense: bfloat16 [32768, 8, 128], P(('dp', 'seq'), 'head'), parts along dimension 0, may hold values from -4 to 4
- v_dense: bfloat16 [32768, 8, 128], P(('dp', 'seq'), 'head'), parts along dimension 0, may hold values from -4 to 4
- q_expert: bfloat16 [32768, 12, 128], P(('dp', 'seq'), 'head'), parts along dimension 0, may hold values from -108 to 108
- k_expert: bfloat16 [32768, 12, 128], P(('dp', 'seq'), 'head'), parts along dimension 0, may hold values from -4 to 4
- v_expert: bfloat16 [32768, 12, 128], P(('dp', 'seq'), 'head'), parts along dimension 0, may hold values from -4 to 4
- gate_logit: bfloat16 [12, 32768], P('head', ('dp', 'seq')), parts along dimension 1, may hold values from -8 to 8
- selection: int32 [12, 2048], P('head', 'dp'), parts along dimension 1, may hold values from 0 to 8191, as said below
Outputs:
- dense_out: bfloat16 [32768, 8, 128], P(('dp', 'seq'), 'head'), parts along dimension 0
- expert_out: bfloat16 [32768, 12, 128], P(('dp', 'seq'), 'head'), parts along dimension 0
The draws below stay inside these ranges and needn't reach their ends.
There are 4 independent parts, one for each index of `dp`. The reference program is written for one: setup_inputs(seed, part) draws one part's arguments, and reference() takes and returns one part's arrays. A program takes and returns all parts, laid end to end along the dimension named above; each array names one. Nothing has to cross between parts.
Inputs may be any that keep to these rules, and one draw needn't show every extreme that they name: `selection`: each row lists 512 distinct token positions in increasing order; every row holds the first and the last token.
All inputs are finite; a program needn't handle non-finite values.
Results may differ from the reference program's by a relative error of at most 0.0055.
Values may be sent and summed in bfloat16 or wider, within the bound.
No kernel may reach another device: no remote copies, remote signals or barrier semaphores. Data moves between devices by JAX's collectives and lax.ppermute only.
A program may use at most 64 MiB of HBM per device.

```python
import math
import jax
import jax.numpy as jnp
from jax import lax

HS = 128
TOK_DEV = 512
DH = 8
EH = 12
TOKENS = 8192
SEL = 512


def choose_tokens(key):
    noise = jax.random.randint(jax.random.fold_in(key, 101), (EH, TOKENS), 0, 1024)
    blocks = TOKENS // TOK_DEV
    raised = jax.random.randint(jax.random.fold_in(key, 102), (EH, blocks), 0, 4) * 512
    raised = jnp.repeat(raised, TOK_DEV, axis=1, total_repeat_length=TOKENS)
    places = jnp.arange(TOKENS, dtype=jnp.int32)
    boundary = jnp.where((places == 0) | (places == TOKENS - 1), 4096, 0)
    score = (noise + raised + boundary[None, :]) * TOKENS + places[None, :]
    leading = jax.lax.top_k(score, SEL)[0]
    return jnp.sort(leading % TOKENS, axis=1).astype(jnp.int32)


def dense_pair(key):
    shape = (TOKENS, DH, HS)
    keys = jnp.clip(jax.random.normal(jax.random.fold_in(key, 201), shape, jnp.float32), -4.0, 4.0)
    query = jnp.clip(jax.random.normal(jax.random.fold_in(key, 202), shape, jnp.float32), -4.0, 4.0)
    return (query, keys)


def expert_pair(key):
    shape = (TOKENS, EH, HS)
    keys = jnp.clip(jax.random.normal(jax.random.fold_in(key, 301), shape, jnp.float32), -4.0, 4.0)
    query = jnp.clip(jax.random.normal(jax.random.fold_in(key, 302), shape, jnp.float32), -4.0, 4.0)
    return (query, keys)


def draw_q_dense(key, part):
    return dense_pair(key)[0].astype(jnp.bfloat16)


def draw_k_dense(key, part):
    return dense_pair(key)[1].astype(jnp.bfloat16)


def draw_q_expert(key, part):
    return expert_pair(key)[0].astype(jnp.bfloat16)


def draw_k_expert(key, part):
    return expert_pair(key)[1].astype(jnp.bfloat16)


def draw_selection(key, part):
    return choose_tokens(key)


def shard_levels(own_key, extent, cuts, least, high):
    def one(position, shards_of):
        heights = jax.random.uniform(jax.random.fold_in(jax.random.fold_in(own_key, 6), position), (shards_of,), jnp.float32, least / len(cuts), high / len(cuts))
        return jnp.repeat(jnp.exp(heights), extent[position] // shards_of).reshape((-1,) + (1,) * (len(extent) - position - 1))

    level = one(*cuts[0])
    for cut in cuts[1:]:
        level = level * one(*cut)
    return level


def normal_values(own_key, extent, spread, limit, cuts=(), kind=jnp.bfloat16):
    array = spread * jax.random.normal(own_key, extent, jnp.float32)
    if cuts:
        array = array * shard_levels(own_key, extent, cuts, -0.22, 0.18)
    return jnp.clip(array, -limit, limit).astype(kind)


def setup_inputs(seed: int = 0, part: int = 0) -> dict:
    key_list = jax.random.split(jax.random.key(seed), 9)
    own_keys = jax.random.split(jax.random.fold_in(key_list[8], part), 9)
    return {
        "q_dense": draw_q_dense(jax.random.fold_in(jax.random.fold_in(key_list[8], part), 71), part),
        "k_dense": draw_k_dense(jax.random.fold_in(jax.random.fold_in(key_list[8], part), 71), part),
        "v_dense": normal_values(own_keys[2], (TOKENS, DH, HS), 1.0, 4.0, ((0, 16), (1, 4))),
        "q_expert": draw_q_expert(jax.random.fold_in(jax.random.fold_in(key_list[8], part), 71), part),
        "k_expert": draw_k_expert(jax.random.fold_in(jax.random.fold_in(key_list[8], part), 71), part),
        "v_expert": normal_values(own_keys[5], (TOKENS, EH, HS), 1.0, 4.0, ((0, 16), (1, 4))),
        "gate_logit": normal_values(own_keys[6], (EH, TOKENS), 2.0, 8.0, ((0, 4), (1, 16))),
        "selection": draw_selection(jax.random.fold_in(jax.random.fold_in(key_list[8], part), 71), part),
    }


NEGATIVE = -1e+30

def attend(queries, query_rank, keys, values, key_rank):
    scores = jnp.dot(queries, keys.T, preferred_element_type=jnp.float32) * (1.0 / math.sqrt(HS))
    visible = key_rank[None, :] <= query_rank[:, None]
    scores = jnp.where(visible, scores, NEGATIVE)
    leading = lax.optimization_barrier(jnp.max(scores, axis=1, keepdims=True))
    weights = jnp.where(visible, jnp.exp(scores - leading), 0.0)
    total = lax.optimization_barrier(jnp.sum(weights, axis=1, keepdims=True))
    mixed = jnp.dot(weights.astype(jnp.bfloat16), values, preferred_element_type=jnp.float32)
    return mixed / total

def dense_head(queries, keys, values):
    block = math.gcd(TOKENS, 512)
    ranks = jnp.arange(TOKENS, dtype=jnp.int32)

    def one_block(index):
        offset = index * block
        part_q = lax.dynamic_slice_in_dim(queries, offset, block, 0)
        part_rank = lax.dynamic_slice_in_dim(ranks, offset, block, 0)
        return attend(part_q, part_rank, keys, values, ranks).astype(jnp.bfloat16)
    blocks = lax.map(one_block, jnp.arange(TOKENS // block, dtype=jnp.int32))
    return blocks.reshape(TOKENS, HS)

def reference(q_dense, k_dense, v_dense, q_expert, k_expert, v_expert, gate_logit, selection):
    dense_out = jnp.stack([dense_head(q_dense[:, head], k_dense[:, head], v_dense[:, head]) for head in range(DH)], axis=1)
    expert_out = jnp.zeros((TOKENS, EH, HS), jnp.bfloat16)
    ranks = jnp.arange(SEL, dtype=jnp.int32)
    for head in range(EH):
        chosen = selection[head]
        mixed = attend(q_expert[chosen, head], ranks, k_expert[chosen, head], v_expert[chosen, head], ranks)
        gate = jax.nn.sigmoid(gate_logit[head, chosen].astype(jnp.float32))
        expert_out = expert_out.at[chosen, head].set((mixed * gate[:, None]).astype(jnp.bfloat16))
    return (dense_out, expert_out)
```

```python
import functools
import math

import jax
import jax.numpy as jnp
from jax import lax
from jax.experimental import pallas as pl
from jax.experimental.pallas import tpu as pltpu
from jax.sharding import PartitionSpec as P

NEGATIVE = -1e30


def flash_kernel(count_ref, q_ref, k_ref, v_ref, o_ref, m_ref, l_ref, acc_ref, *, scale, blocks):
    step = pl.program_id(1)
    last = count_ref[0]

    @pl.when(step == 0)
    def _():
        m_ref[...] = jnp.full(m_ref.shape, NEGATIVE, jnp.float32)
        l_ref[...] = jnp.zeros(l_ref.shape, jnp.float32)
        acc_ref[...] = jnp.zeros(acc_ref.shape, jnp.float32)

    @pl.when(step <= last)
    def _():
        q = q_ref[0]
        k = k_ref[0]
        scores = lax.dot_general(
            q, k, (((1,), (1,)), ((), ())), preferred_element_type=jnp.float32
        ) * scale
        rows = lax.broadcasted_iota(jnp.int32, scores.shape, 0)
        cols = lax.broadcasted_iota(jnp.int32, scores.shape, 1)
        visible = (cols <= rows) | (step < last)
        scores = jnp.where(visible, scores, NEGATIVE)
        m_prev = m_ref[:, :1]
        m_new = jnp.maximum(m_prev, jnp.max(scores, axis=1, keepdims=True))
        shrink = jnp.exp(m_prev - m_new)
        weights = jnp.where(visible, jnp.exp(scores - m_new), 0.0)
        l_new = l_ref[:, :1] * shrink + jnp.sum(weights, axis=1, keepdims=True)
        moved = jnp.dot(weights.astype(jnp.bfloat16), v_ref[0], preferred_element_type=jnp.float32)
        acc_ref[...] = acc_ref[...] * shrink + moved
        m_ref[...] = jnp.broadcast_to(m_new, m_ref.shape)
        l_ref[...] = jnp.broadcast_to(l_new, l_ref.shape)

    @pl.when(step == blocks - 1)
    def _():
        o_ref[0] = (acc_ref[...] / l_ref[:, :1]).astype(o_ref.dtype)


def dense_flash(count, queries, keys, values):
    heads, rows, width = queries.shape
    blocks = keys.shape[1] // rows
    scale = 1.0 / math.sqrt(width)

    def kv_map(h, j, c):
        return (h, jnp.minimum(j, c[0]), 0)

    return pl.pallas_call(
        functools.partial(flash_kernel, scale=scale, blocks=blocks),
        out_shape=jax.ShapeDtypeStruct((heads, rows, width), jnp.bfloat16),
        grid_spec=pltpu.PrefetchScalarGridSpec(
            num_scalar_prefetch=1,
            grid=(heads, blocks),
            in_specs=[
                pl.BlockSpec((1, rows, width), lambda h, j, c: (h, 0, 0)),
                pl.BlockSpec((1, rows, width), kv_map),
                pl.BlockSpec((1, rows, width), kv_map),
            ],
            out_specs=pl.BlockSpec((1, rows, width), lambda h, j, c: (h, 0, 0)),
            scratch_shapes=[
                pltpu.VMEM((rows, 128), jnp.float32),
                pltpu.VMEM((rows, 128), jnp.float32),
                pltpu.VMEM((rows, width), jnp.float32),
            ],
        ),
        compiler_params=pltpu.CompilerParams(dimension_semantics=("arbitrary", "arbitrary")),
        cost_estimate=pl.CostEstimate(
            flops=4 * heads * rows * keys.shape[1] * width,
            transcendentals=heads * rows * keys.shape[1],
            bytes_accessed=2 * (2 * keys.size + 2 * queries.size),
        ),
    )(count, queries, keys, values)


def dense_heads(queries, keys, values):
    tok_rows, heads, width = queries.shape
    stacked = jnp.stack([jnp.swapaxes(keys, 0, 1), jnp.swapaxes(values, 0, 1)], axis=0)
    gathered = lax.all_gather(stacked, "seq", axis=2, tiled=True)
    count = lax.axis_index("seq").astype(jnp.int32).reshape(1)
    out = dense_flash(count, jnp.swapaxes(queries, 0, 1), gathered[0], gathered[1])
    return jnp.swapaxes(out, 0, 1)


def attend_ranked(query_rows, keys, values, gate_rows):
    heads, rows, width = query_rows.shape
    scale = 1.0 / math.sqrt(width)
    ranks = jnp.arange(rows, dtype=jnp.int32)
    scores = jnp.einsum("erd,ekd->erk", query_rows, keys, preferred_element_type=jnp.float32) * scale
    visible = ranks[None, None, :] <= ranks[None, :, None]
    scores = jnp.where(visible, scores, NEGATIVE)
    leading = jnp.max(scores, axis=2, keepdims=True)
    weights = jnp.where(visible, jnp.exp(scores - leading), 0.0)
    total = jnp.sum(weights, axis=2, keepdims=True)
    mixed = (
        jnp.einsum("erk,ekd->erd", weights.astype(jnp.bfloat16), values, preferred_element_type=jnp.float32)
        / total
    )
    return (mixed * jax.nn.sigmoid(gate_rows)[:, :, None]).astype(jnp.bfloat16)


def sparse_heads(queries, keys, values, gate_logit, selection):
    tok_rows, heads, width = queries.shape
    start = lax.axis_index("seq") * tok_rows
    positions = start + jnp.arange(tok_rows, dtype=jnp.int32)
    one_hot = (selection[:, :, None] == positions[None, None, :]).astype(jnp.bfloat16)

    def pick(source):
        return jnp.einsum("ent,ted->end", one_hot, source, preferred_element_type=jnp.float32).astype(
            jnp.bfloat16
        )

    local_kv = jnp.stack([pick(keys), pick(values)], axis=0)
    picked_kv = lax.psum(local_kv, "seq")
    picked_q = pick(queries)
    gate_rows = jnp.einsum("ent,et->en", one_hot, gate_logit, preferred_element_type=jnp.float32)
    results = attend_ranked(picked_q, picked_kv[0], picked_kv[1], gate_rows)
    return jnp.einsum("ent,end->ted", one_hot, results, preferred_element_type=jnp.float32).astype(
        jnp.bfloat16
    )


def local(q_dense, k_dense, v_dense, q_expert, k_expert, v_expert, gate_logit, selection):
    dense_out = dense_heads(q_dense, k_dense, v_dense)
    expert_out = sparse_heads(q_expert, k_expert, v_expert, gate_logit, selection)
    return (dense_out, expert_out)


def solution(mesh):
    rows = P(("dp", "seq"), "head", None)
    placed = (rows, rows, rows, rows, rows, rows, P("head", ("dp", "seq")), P("head", "dp"))
    return jax.shard_map(
        local,
        mesh=mesh,
        in_specs=placed,
        out_specs=(rows, rows),
        check_vma=False,
    )
```

```python
import functools
import math

import jax
import jax.numpy as jnp
from jax import lax
from jax.experimental import pallas as pl
from jax.experimental.pallas import tpu as pltpu
from jax.sharding import PartitionSpec as P

NEGATIVE = -1e30


def flash_kernel(count_ref, q_ref, k_ref, v_ref, o_ref, m_ref, l_ref, acc_ref, *, scale, blocks):
    step = pl.program_id(1)
    last = count_ref[0]

    @pl.when(step == 0)
    def _():
        m_ref[...] = jnp.full(m_ref.shape, NEGATIVE, jnp.float32)
        l_ref[...] = jnp.zeros(l_ref.shape, jnp.float32)
        acc_ref[...] = jnp.zeros(acc_ref.shape, jnp.float32)

    @pl.when(step <= last)
    def _():
        q = q_ref[0]
        k = k_ref[0]
        scores = lax.dot_general(
            q, k, (((1,), (1,)), ((), ())), preferred_element_type=jnp.float32
        ) * scale
        rows = lax.broadcasted_iota(jnp.int32, scores.shape, 0)
        cols = lax.broadcasted_iota(jnp.int32, scores.shape, 1)
        visible = (cols <= rows) | (step < last)
        scores = jnp.where(visible, scores, NEGATIVE)
        m_prev = m_ref[:, :1]
        m_new = jnp.maximum(m_prev, jnp.max(scores, axis=1, keepdims=True))
        shrink = jnp.exp(m_prev - m_new)
        weights = jnp.where(visible, jnp.exp(scores - m_new), 0.0)
        l_new = l_ref[:, :1] * shrink + jnp.sum(weights, axis=1, keepdims=True)
        moved = jnp.dot(weights.astype(jnp.bfloat16), v_ref[0], preferred_element_type=jnp.float32)
        acc_ref[...] = acc_ref[...] * shrink + moved
        m_ref[...] = jnp.broadcast_to(m_new, m_ref.shape)
        l_ref[...] = jnp.broadcast_to(l_new, l_ref.shape)

    @pl.when(step == blocks - 1)
    def _():
        o_ref[0] = (acc_ref[...] / l_ref[:, :1]).astype(o_ref.dtype)


def dense_flash(count, queries, stacked):
    heads, rows, width = queries.shape
    length = stacked.shape[2]
    blocks = length // rows
    scale = 1.0 / math.sqrt(width)

    def kv_map(which):
        return lambda h, j, c: (which, h, jnp.minimum(j, c[0]), 0)

    return pl.pallas_call(
        functools.partial(flash_kernel, scale=scale, blocks=blocks),
        out_shape=jax.ShapeDtypeStruct((heads, rows, width), jnp.bfloat16),
        grid_spec=pltpu.PrefetchScalarGridSpec(
            num_scalar_prefetch=1,
            grid=(heads, blocks),
            in_specs=[
                pl.BlockSpec((1, rows, width), lambda h, j, c: (h, 0, 0)),
                pl.BlockSpec((None, 1, rows, width), kv_map(0)),
                pl.BlockSpec((None, 1, rows, width), kv_map(1)),
            ],
            out_specs=pl.BlockSpec((1, rows, width), lambda h, j, c: (h, 0, 0)),
            scratch_shapes=[
                pltpu.VMEM((rows, 128), jnp.float32),
                pltpu.VMEM((rows, 128), jnp.float32),
                pltpu.VMEM((rows, width), jnp.float32),
            ],
        ),
        compiler_params=pltpu.CompilerParams(dimension_semantics=("arbitrary", "arbitrary")),
        cost_estimate=pl.CostEstimate(
            flops=4 * heads * rows * length * width,
            transcendentals=heads * rows * length,
            bytes_accessed=2 * (stacked.size + 2 * queries.size),
        ),
    )(count, queries, stacked, stacked)


def dense_heads(queries, keys, values):
    tok_rows, heads, width = queries.shape
    stacked = jnp.stack([jnp.swapaxes(keys, 0, 1), jnp.swapaxes(values, 0, 1)], axis=0)
    gathered = lax.all_gather(stacked, "seq", axis=2, tiled=True)
    count = lax.axis_index("seq").astype(jnp.int32).reshape(1)
    out = dense_flash(count, jnp.swapaxes(queries, 0, 1), gathered)
    return jnp.swapaxes(out, 0, 1)


def attend_ranked(query_rows, keys, values, gate_rows):
    heads, rows, width = query_rows.shape
    scale = 1.0 / math.sqrt(width)
    ranks = jnp.arange(rows, dtype=jnp.int32)
    scores = jnp.einsum("erd,ekd->erk", query_rows, keys, preferred_element_type=jnp.float32) * scale
    visible = ranks[None, None, :] <= ranks[None, :, None]
    scores = jnp.where(visible, scores, NEGATIVE)
    leading = jnp.max(scores, axis=2, keepdims=True)
    weights = jnp.where(visible, jnp.exp(scores - leading), 0.0)
    total = jnp.sum(weights, axis=2, keepdims=True)
    mixed = (
        jnp.einsum("erk,ekd->erd", weights.astype(jnp.bfloat16), values, preferred_element_type=jnp.float32)
        / total
    )
    return (mixed * jax.nn.sigmoid(gate_rows)[:, :, None]).astype(jnp.bfloat16)


def sparse_heads(queries, keys, values, gate_logit, selection):
    tok_rows, heads, width = queries.shape
    start = lax.axis_index("seq") * tok_rows
    positions = start + jnp.arange(tok_rows, dtype=jnp.int32)
    one_hot = (selection[:, :, None] == positions[None, None, :]).astype(jnp.bfloat16)

    def pick(source):
        return jnp.einsum("ent,ted->end", one_hot, source, preferred_element_type=jnp.float32).astype(
            jnp.bfloat16
        )

    count = lax.axis_size("seq")
    local_kv = jnp.stack([pick(keys), pick(values)], axis=0)
    kinds, heads_, chosen, width_ = local_kv.shape
    pieces = local_kv.reshape(kinds, heads_, count, chosen // count, width_)
    arrived = lax.all_to_all(pieces, "seq", 2, 2, tiled=True)
    own = jnp.sum(arrived.astype(jnp.float32), axis=2).astype(jnp.bfloat16)
    picked_kv = lax.all_gather(own, "seq", axis=2, tiled=True)
    picked_q = pick(queries)
    gate_rows = jnp.einsum("ent,et->en", one_hot, gate_logit, preferred_element_type=jnp.float32)
    results = attend_ranked(picked_q, picked_kv[0], picked_kv[1], gate_rows)
    return jnp.einsum("ent,end->ted", one_hot, results, preferred_element_type=jnp.float32).astype(
        jnp.bfloat16
    )


def local(q_dense, k_dense, v_dense, q_expert, k_expert, v_expert, gate_logit, selection):
    dense_out = dense_heads(q_dense, k_dense, v_dense)
    expert_out = sparse_heads(q_expert, k_expert, v_expert, gate_logit, selection)
    return (dense_out, expert_out)


def solution(mesh):
    rows = P(("dp", "seq"), "head", None)
    placed = (rows, rows, rows, rows, rows, rows, P("head", ("dp", "seq")), P("head", "dp"))
    return jax.shard_map(
        local,
        mesh=mesh,
        in_specs=placed,
        out_specs=(rows, rows),
        check_vma=False,
    )
```

```python
import functools
import math

import jax
import jax.numpy as jnp
from jax import lax
from jax.experimental import pallas as pl
from jax.experimental.pallas import tpu as pltpu
from jax.sharding import PartitionSpec as P

NEGATIVE = -1e30


def flash_kernel(info_ref, q_ref, k_ref, v_ref, o_ref, m_ref, l_ref, acc_ref, *, scale, blocks):
    part = pl.program_id(1)
    step = pl.program_id(2)
    last = info_ref[part]
    offset = info_ref[2 + part]

    @pl.when(step == 0)
    def _():
        m_ref[...] = jnp.full(m_ref.shape, NEGATIVE, jnp.float32)
        l_ref[...] = jnp.zeros(l_ref.shape, jnp.float32)
        acc_ref[...] = jnp.zeros(acc_ref.shape, jnp.float32)

    def update(masked):
        scores = lax.dot_general(
            q_ref[0, 0], k_ref[0], (((1,), (1,)), ((), ())), preferred_element_type=jnp.float32
        ) * scale
        if masked:
            rows = lax.broadcasted_iota(jnp.int32, scores.shape, 0) + offset
            cols = lax.broadcasted_iota(jnp.int32, scores.shape, 1)
            scores = jnp.where(cols <= rows, scores, NEGATIVE)
        m_prev = m_ref[:, :1]
        m_new = jnp.maximum(m_prev, jnp.max(scores, axis=1, keepdims=True))
        shrink = jnp.exp(m_prev - m_new)
        weights = jnp.exp(scores - m_new)
        l_new = l_ref[:, :1] * shrink + jnp.sum(weights, axis=1, keepdims=True)
        moved = jnp.dot(weights.astype(jnp.bfloat16), v_ref[0], preferred_element_type=jnp.float32)
        acc_ref[...] = acc_ref[...] * shrink + moved
        m_ref[...] = jnp.broadcast_to(m_new, m_ref.shape)
        l_ref[...] = jnp.broadcast_to(l_new, l_ref.shape)

    @pl.when(step < last)
    def _():
        update(False)

    @pl.when(step == last)
    def _():
        update(True)

    @pl.when(step == blocks - 1)
    def _():
        o_ref[0, 0] = (acc_ref[...] / l_ref[:, :1]).astype(o_ref.dtype)


def dense_flash(info, queries, stacked):
    parts, heads, rows, width = queries.shape
    length = stacked.shape[2]
    block = 512
    blocks = length // block
    scale = 1.0 / math.sqrt(width)

    def kv_map(which):
        return lambda h, p, j, c: (which, h, jnp.minimum(j, c[p]), 0)

    return pl.pallas_call(
        functools.partial(flash_kernel, scale=scale, blocks=blocks),
        out_shape=jax.ShapeDtypeStruct((parts, heads, rows, width), jnp.bfloat16),
        grid_spec=pltpu.PrefetchScalarGridSpec(
            num_scalar_prefetch=1,
            grid=(heads, parts, blocks),
            in_specs=[
                pl.BlockSpec((1, 1, rows, width), lambda h, p, j, c: (p, h, 0, 0)),
                pl.BlockSpec((None, 1, block, width), kv_map(0)),
                pl.BlockSpec((None, 1, block, width), kv_map(1)),
            ],
            out_specs=pl.BlockSpec((1, 1, rows, width), lambda h, p, j, c: (p, h, 0, 0)),
            scratch_shapes=[
                pltpu.VMEM((rows, 128), jnp.float32),
                pltpu.VMEM((rows, 128), jnp.float32),
                pltpu.VMEM((rows, width), jnp.float32),
            ],
        ),
        compiler_params=pltpu.CompilerParams(
            dimension_semantics=("arbitrary", "arbitrary", "arbitrary")
        ),
        cost_estimate=pl.CostEstimate(
            flops=2 * heads * rows * length * width,
            transcendentals=heads * rows * length // 2,
            bytes_accessed=stacked.size + 4 * queries.size,
        ),
    )(info, queries, stacked, stacked)


def dense_heads(queries, keys, values):
    tok_rows, heads, width = queries.shape
    count = lax.axis_size("seq")
    me = lax.axis_index("seq").astype(jnp.int32)
    partner = count - 1 - me
    half = tok_rows // 2
    swap = [(i, count - 1 - i) for i in range(count)]
    stacked = jnp.stack([jnp.swapaxes(keys, 0, 1), jnp.swapaxes(values, 0, 1)], axis=0)
    gathered = lax.all_gather(stacked, "seq", axis=2, tiled=True)
    rows_first = jnp.swapaxes(queries, 0, 1)
    lent = lax.ppermute(rows_first[:, half:], "seq", swap)
    both = jnp.stack([rows_first[:, :half], lent], axis=0)
    info = jnp.stack([me, partner, jnp.int32(0), jnp.int32(half)])
    out = dense_flash(info, both, gathered)
    returned = lax.ppermute(out[1], "seq", swap)
    mine = jnp.concatenate([out[0], returned], axis=1)
    return jnp.swapaxes(mine, 0, 1)


def attend_ranked(query_rows, keys, values, gate_rows):
    heads, rows, width = query_rows.shape
    scale = 1.0 / math.sqrt(width)
    ranks = jnp.arange(rows, dtype=jnp.int32)
    scores = jnp.einsum("erd,ekd->erk", query_rows, keys, preferred_element_type=jnp.float32) * scale
    visible = ranks[None, None, :] <= ranks[None, :, None]
    scores = jnp.where(visible, scores, NEGATIVE)
    leading = jnp.max(scores, axis=2, keepdims=True)
    weights = jnp.where(visible, jnp.exp(scores - leading), 0.0)
    total = jnp.sum(weights, axis=2, keepdims=True)
    mixed = (
        jnp.einsum("erk,ekd->erd", weights.astype(jnp.bfloat16), values, preferred_element_type=jnp.float32)
        / total
    )
    return (mixed * jax.nn.sigmoid(gate_rows)[:, :, None]).astype(jnp.bfloat16)


def sparse_heads(queries, keys, values, gate_logit, selection):
    tok_rows, heads, width = queries.shape
    start = lax.axis_index("seq") * tok_rows
    positions = start + jnp.arange(tok_rows, dtype=jnp.int32)
    one_hot = (selection[:, :, None] == positions[None, None, :]).astype(jnp.bfloat16)

    def pick(source):
        return jnp.einsum("ent,ted->end", one_hot, source, preferred_element_type=jnp.float32).astype(
            jnp.bfloat16
        )

    count = lax.axis_size("seq")
    local_kv = jnp.stack([pick(keys), pick(values)], axis=0)
    kinds, heads_, chosen, width_ = local_kv.shape
    pieces = local_kv.reshape(kinds, heads_, count, chosen // count, width_)
    arrived = lax.all_to_all(pieces, "seq", 2, 2, tiled=True)
    own = jnp.sum(arrived.astype(jnp.float32), axis=2).astype(jnp.bfloat16)
    picked_kv = lax.all_gather(own, "seq", axis=2, tiled=True)
    picked_q = pick(queries)
    gate_rows = jnp.einsum("ent,et->en", one_hot, gate_logit, preferred_element_type=jnp.float32)
    results = attend_ranked(picked_q, picked_kv[0], picked_kv[1], gate_rows)
    return jnp.einsum("ent,end->ted", one_hot, results, preferred_element_type=jnp.float32).astype(
        jnp.bfloat16
    )


def local(q_dense, k_dense, v_dense, q_expert, k_expert, v_expert, gate_logit, selection):
    dense_out = dense_heads(q_dense, k_dense, v_dense)
    expert_out = sparse_heads(q_expert, k_expert, v_expert, gate_logit, selection)
    return (dense_out, expert_out)


def solution(mesh):
    rows = P(("dp", "seq"), "head", None)
    placed = (rows, rows, rows, rows, rows, rows, P("head", ("dp", "seq")), P("head", "dp"))
    return jax.shard_map(
        local,
        mesh=mesh,
        in_specs=placed,
        out_specs=(rows, rows),
        check_vma=False,
    )
```

```python
import functools
import math

import jax
import jax.numpy as jnp
from jax import lax
from jax.experimental import pallas as pl
from jax.experimental.pallas import tpu as pltpu
from jax.sharding import PartitionSpec as P

NEGATIVE = -1e30


def flash_kernel(info_ref, q_ref, m_in, l_in, acc_in, *refs, scale, count):
    kv_refs = refs[: 2 * count]
    m_out, l_out, acc_out = refs[2 * count :]
    part = pl.program_id(1)
    last = info_ref[part]
    offset = info_ref[2 + part]
    m_out[0, 0] = m_in[0, 0]
    l_out[0, 0] = l_in[0, 0]
    acc_out[0, 0] = acc_in[0, 0]

    def update(k_ref, v_ref, masked):
        scores = lax.dot_general(
            q_ref[0, 0], k_ref[0], (((1,), (1,)), ((), ())), preferred_element_type=jnp.float32
        ) * scale
        if masked:
            rows = lax.broadcasted_iota(jnp.int32, scores.shape, 0) + offset
            cols = lax.broadcasted_iota(jnp.int32, scores.shape, 1)
            scores = jnp.where(cols <= rows, scores, NEGATIVE)
        m_prev = m_out[0, 0][:, :1]
        m_new = jnp.maximum(m_prev, jnp.max(scores, axis=1, keepdims=True))
        shrink = jnp.exp(m_prev - m_new)
        weights = jnp.exp(scores - m_new)
        l_new = l_out[0, 0][:, :1] * shrink + jnp.sum(weights, axis=1, keepdims=True)
        moved = jnp.dot(weights.astype(jnp.bfloat16), v_ref[0], preferred_element_type=jnp.float32)
        acc_out[0, 0] = acc_out[0, 0] * shrink + moved
        m_out[0, 0] = jnp.broadcast_to(m_new, m_out.shape[2:])
        l_out[0, 0] = jnp.broadcast_to(l_new, l_out.shape[2:])

    for b in range(count):
        index = info_ref[4 + b]

        @pl.when(index < last)
        def _():
            update(kv_refs[2 * b], kv_refs[2 * b + 1], False)

        @pl.when(index == last)
        def _():
            update(kv_refs[2 * b], kv_refs[2 * b + 1], True)


def flash_round(info, queries, state, blocks):
    parts, heads, rows, width = queries.shape
    block = blocks[0].shape[2]
    count = len(blocks)
    scale = 1.0 / math.sqrt(width)
    row_spec = pl.BlockSpec((1, 1, rows, width), lambda h, p, c: (p, h, 0, 0))
    kv_specs = []
    kv_args = []
    for item in blocks:
        for which in range(2):
            kv_specs.append(pl.BlockSpec((None, 1, block, width), lambda h, p, c, w=which: (w, h, 0, 0)))
            kv_args.append(item)
    return pl.pallas_call(
        functools.partial(flash_kernel, scale=scale, count=count),
        out_shape=[jax.ShapeDtypeStruct(x.shape, x.dtype) for x in state],
        grid_spec=pltpu.PrefetchScalarGridSpec(
            num_scalar_prefetch=1,
            grid=(heads, parts),
            in_specs=[row_spec, row_spec, row_spec, row_spec] + kv_specs,
            out_specs=[row_spec, row_spec, row_spec],
        ),
        input_output_aliases={2: 0, 3: 1, 4: 2},
        compiler_params=pltpu.CompilerParams(dimension_semantics=("arbitrary", "arbitrary")),
        cost_estimate=pl.CostEstimate(
            flops=4 * heads * parts * rows * block * width * count // 2,
            transcendentals=heads * parts * rows * block * count // 2,
            bytes_accessed=2 * count * blocks[0].size + 12 * queries.size,
        ),
    )(info, queries, *state, *kv_args)


def dense_heads(queries, keys, values):
    tok_rows, heads, width = queries.shape
    count = lax.axis_size("seq")
    chips = count // 2
    me = lax.axis_index("seq").astype(jnp.int32)
    partner = count - 1 - me
    half = tok_rows // 2
    swap = [(i, count - 1 - i) for i in range(count)]
    up = [(i, (i + 2) % count) for i in range(count)]
    down = [(i, (i - 2) % count) for i in range(count)]
    sib = [(i, i ^ 1) for i in range(count)]
    own = jnp.stack([jnp.swapaxes(keys, 0, 1), jnp.swapaxes(values, 0, 1)], axis=0)
    rows_first = jnp.swapaxes(queries, 0, 1)
    lent = lax.ppermute(rows_first[:, half:], "seq", swap)
    both = jnp.stack([rows_first[:, :half], lent], axis=0)
    head = jnp.stack([me, partner, jnp.int32(0), jnp.int32(half)])
    state = (
        jnp.full((2, heads, half, 128), NEGATIVE, jnp.float32),
        jnp.zeros((2, heads, half, 128), jnp.float32),
        jnp.zeros((2, heads, half, width), jnp.float32),
    )

    def run(state, items):
        info = jnp.concatenate([head, jnp.stack([index for index, _ in items])])
        return flash_round(info, both, state, [item for _, item in items])

    pending = [(me ^ 1, lax.ppermute(own, "seq", sib))]
    state = run(state, [(me, own)])
    cur_up, cur_dn = own, own
    for t in range(1, chips // 2 + 1):
        cur_up = lax.ppermute(cur_up, "seq", up)
        arrived = [((me - 2 * t) % count, cur_up)]
        if 2 * t < chips:
            cur_dn = lax.ppermute(cur_dn, "seq", down)
            arrived.append(((me + 2 * t) % count, cur_dn))
        sent = [(index ^ 1, lax.ppermute(item, "seq", sib)) for index, item in arrived]
        state = run(state, pending + arrived)
        pending = sent
    state = run(state, pending)
    m_final, l_final, acc_final = state
    out = (acc_final / l_final[..., :1]).astype(jnp.bfloat16)
    returned = lax.ppermute(out[1], "seq", swap)
    mine = jnp.concatenate([out[0], returned], axis=1)
    return jnp.swapaxes(mine, 0, 1)


def attend_ranked(query_rows, keys, values, gate_rows):
    heads, rows, width = query_rows.shape
    scale = 1.0 / math.sqrt(width)
    ranks = jnp.arange(rows, dtype=jnp.int32)
    scores = jnp.einsum("erd,ekd->erk", query_rows, keys, preferred_element_type=jnp.float32) * scale
    visible = ranks[None, None, :] <= ranks[None, :, None]
    scores = jnp.where(visible, scores, NEGATIVE)
    leading = jnp.max(scores, axis=2, keepdims=True)
    weights = jnp.where(visible, jnp.exp(scores - leading), 0.0)
    total = jnp.sum(weights, axis=2, keepdims=True)
    mixed = (
        jnp.einsum("erk,ekd->erd", weights.astype(jnp.bfloat16), values, preferred_element_type=jnp.float32)
        / total
    )
    return (mixed * jax.nn.sigmoid(gate_rows)[:, :, None]).astype(jnp.bfloat16)


def sparse_heads(queries, keys, values, gate_logit, selection):
    tok_rows, heads, width = queries.shape
    start = lax.axis_index("seq") * tok_rows
    positions = start + jnp.arange(tok_rows, dtype=jnp.int32)
    one_hot = (selection[:, :, None] == positions[None, None, :]).astype(jnp.bfloat16)

    def pick(source):
        return jnp.einsum("ent,ted->end", one_hot, source, preferred_element_type=jnp.float32).astype(
            jnp.bfloat16
        )

    count = lax.axis_size("seq")
    local_kv = jnp.stack([pick(keys), pick(values)], axis=0)
    kinds, heads_, chosen, width_ = local_kv.shape
    pieces = local_kv.reshape(kinds, heads_, count, chosen // count, width_)
    arrived = lax.all_to_all(pieces, "seq", 2, 2, tiled=True)
    own = jnp.sum(arrived.astype(jnp.float32), axis=2).astype(jnp.bfloat16)
    picked_kv = lax.all_gather(own, "seq", axis=2, tiled=True)
    picked_q = pick(queries)
    gate_rows = jnp.einsum("ent,et->en", one_hot, gate_logit, preferred_element_type=jnp.float32)
    results = attend_ranked(picked_q, picked_kv[0], picked_kv[1], gate_rows)
    return jnp.einsum("ent,end->ted", one_hot, results, preferred_element_type=jnp.float32).astype(
        jnp.bfloat16
    )


def local(q_dense, k_dense, v_dense, q_expert, k_expert, v_expert, gate_logit, selection):
    dense_out = dense_heads(q_dense, k_dense, v_dense)
    expert_out = sparse_heads(q_expert, k_expert, v_expert, gate_logit, selection)
    return (dense_out, expert_out)


def solution(mesh):
    rows = P(("dp", "seq"), "head", None)
    placed = (rows, rows, rows, rows, rows, rows, P("head", ("dp", "seq")), P("head", "dp"))
    return jax.shard_map(
        local,
        mesh=mesh,
        in_specs=placed,
        out_specs=(rows, rows),
        check_vma=False,
    )
```

```python
import functools
import math

import jax
import jax.numpy as jnp
from jax import lax
from jax.experimental import pallas as pl
from jax.experimental.pallas import tpu as pltpu
from jax.sharding import PartitionSpec as P

NEGATIVE = -1e30


def flash_kernel(info_ref, q_ref, k_ref, v_ref, o_ref, m_ref, l_ref, acc_ref, *, scale, block):
    last = info_ref[0]
    offset = info_ref[1]
    m_ref[...] = jnp.full(m_ref.shape, NEGATIVE, jnp.float32)
    l_ref[...] = jnp.zeros(l_ref.shape, jnp.float32)
    acc_ref[...] = jnp.zeros(acc_ref.shape, jnp.float32)

    def update(j, masked):
        first = pl.multiple_of(j * block, block)
        scores = lax.dot_general(
            q_ref[0], k_ref[0, pl.ds(first, block), :], (((1,), (1,)), ((), ())),
            preferred_element_type=jnp.float32,
        ) * scale
        if masked:
            rows = lax.broadcasted_iota(jnp.int32, scores.shape, 0) + offset
            cols = lax.broadcasted_iota(jnp.int32, scores.shape, 1)
            scores = jnp.where(cols <= rows, scores, NEGATIVE)
        m_prev = m_ref[:, :1]
        m_new = jnp.maximum(m_prev, jnp.max(scores, axis=1, keepdims=True))
        shrink = jnp.exp(m_prev - m_new)
        weights = jnp.exp(scores - m_new)
        l_new = l_ref[:, :1] * shrink + jnp.sum(weights, axis=1, keepdims=True)
        moved = jnp.dot(
            weights.astype(jnp.bfloat16), v_ref[0, pl.ds(first, block), :],
            preferred_element_type=jnp.float32,
        )
        acc_ref[...] = acc_ref[...] * shrink + moved
        m_ref[...] = jnp.broadcast_to(m_new, m_ref.shape)
        l_ref[...] = jnp.broadcast_to(l_new, l_ref.shape)

    def body(j, carry):
        update(j, False)
        return carry

    lax.fori_loop(0, last, body, 0)
    update(last, True)
    o_ref[0] = (acc_ref[...] / l_ref[:, :1]).astype(o_ref.dtype)


def dense_flash(info, queries, stacked):
    heads, rows, width = queries.shape
    length = stacked.shape[2]
    block = 512
    scale = 1.0 / math.sqrt(width)
    return pl.pallas_call(
        functools.partial(flash_kernel, scale=scale, block=block),
        out_shape=jax.ShapeDtypeStruct((heads, rows, width), jnp.bfloat16),
        grid_spec=pltpu.PrefetchScalarGridSpec(
            num_scalar_prefetch=1,
            grid=(heads,),
            in_specs=[
                pl.BlockSpec((1, rows, width), lambda h, c: (h, 0, 0)),
                pl.BlockSpec((None, 1, length, width), lambda h, c: (0, h, 0, 0)),
                pl.BlockSpec((None, 1, length, width), lambda h, c: (1, h, 0, 0)),
            ],
            out_specs=pl.BlockSpec((1, rows, width), lambda h, c: (h, 0, 0)),
            scratch_shapes=[
                pltpu.VMEM((rows, 128), jnp.float32),
                pltpu.VMEM((rows, 128), jnp.float32),
                pltpu.VMEM((rows, width), jnp.float32),
            ],
        ),
        compiler_params=pltpu.CompilerParams(dimension_semantics=("arbitrary",)),
        cost_estimate=pl.CostEstimate(
            flops=2 * heads * rows * length * width,
            transcendentals=heads * rows * length // 2,
            bytes_accessed=stacked.size + 4 * queries.size,
        ),
    )(info, queries, stacked, stacked)


def dense_heads(queries, keys, values):
    tok_rows, heads, width = queries.shape
    count = lax.axis_size("seq")
    me = lax.axis_index("seq").astype(jnp.int32)
    partner = count - 1 - me
    half = tok_rows // 2
    swap = [(i, count - 1 - i) for i in range(count)]
    stacked = jnp.stack([jnp.swapaxes(keys, 0, 1), jnp.swapaxes(values, 0, 1)], axis=0)
    gathered = lax.all_gather(stacked, "seq", axis=2, tiled=True)
    rows_first = jnp.swapaxes(queries, 0, 1)
    lent = lax.ppermute(rows_first[:, half:], "seq", swap)
    theirs = dense_flash(jnp.stack([partner, jnp.int32(half)]), lent, gathered)
    returned = lax.ppermute(theirs, "seq", swap)
    ours = dense_flash(jnp.stack([me, jnp.int32(0)]), rows_first[:, :half], gathered)
    mine = jnp.concatenate([ours, returned], axis=1)
    return jnp.swapaxes(mine, 0, 1)


def attend_ranked(query_rows, keys, values, gate_rows):
    heads, rows, width = query_rows.shape
    scale = 1.0 / math.sqrt(width)
    ranks = jnp.arange(rows, dtype=jnp.int32)
    scores = jnp.einsum("erd,ekd->erk", query_rows, keys, preferred_element_type=jnp.float32) * scale
    visible = ranks[None, None, :] <= ranks[None, :, None]
    scores = jnp.where(visible, scores, NEGATIVE)
    leading = jnp.max(scores, axis=2, keepdims=True)
    weights = jnp.where(visible, jnp.exp(scores - leading), 0.0)
    total = jnp.sum(weights, axis=2, keepdims=True)
    mixed = (
        jnp.einsum("erk,ekd->erd", weights.astype(jnp.bfloat16), values, preferred_element_type=jnp.float32)
        / total
    )
    return (mixed * jax.nn.sigmoid(gate_rows)[:, :, None]).astype(jnp.bfloat16)


def sparse_heads(queries, keys, values, gate_logit, selection):
    tok_rows, heads, width = queries.shape
    start = lax.axis_index("seq") * tok_rows
    positions = start + jnp.arange(tok_rows, dtype=jnp.int32)
    one_hot = (selection[:, :, None] == positions[None, None, :]).astype(jnp.bfloat16)

    def pick(source):
        return jnp.einsum("ent,ted->end", one_hot, source, preferred_element_type=jnp.float32).astype(
            jnp.bfloat16
        )

    count = lax.axis_size("seq")
    local_kv = jnp.stack([pick(keys), pick(values)], axis=0)
    kinds, heads_, chosen, width_ = local_kv.shape
    pieces = local_kv.reshape(kinds, heads_, count, chosen // count, width_)
    arrived = lax.all_to_all(pieces, "seq", 2, 2, tiled=True)
    own = jnp.sum(arrived.astype(jnp.float32), axis=2).astype(jnp.bfloat16)
    picked_kv = lax.all_gather(own, "seq", axis=2, tiled=True)
    picked_q = pick(queries)
    gate_rows = jnp.einsum("ent,et->en", one_hot, gate_logit, preferred_element_type=jnp.float32)
    results = attend_ranked(picked_q, picked_kv[0], picked_kv[1], gate_rows)
    return jnp.einsum("ent,end->ted", one_hot, results, preferred_element_type=jnp.float32).astype(
        jnp.bfloat16
    )


def local(q_dense, k_dense, v_dense, q_expert, k_expert, v_expert, gate_logit, selection):
    dense_out = dense_heads(q_dense, k_dense, v_dense)
    expert_out = sparse_heads(q_expert, k_expert, v_expert, gate_logit, selection)
    return (dense_out, expert_out)


def solution(mesh):
    rows = P(("dp", "seq"), "head", None)
    placed = (rows, rows, rows, rows, rows, rows, P("head", ("dp", "seq")), P("head", "dp"))
    return jax.shard_map(
        local,
        mesh=mesh,
        in_specs=placed,
        out_specs=(rows, rows),
        check_vma=False,
    )
```

```python
import functools
import math

import jax
import jax.numpy as jnp
from jax import lax
from jax.experimental import pallas as pl
from jax.experimental.pallas import tpu as pltpu
from jax.sharding import PartitionSpec as P

NEGATIVE = -1e30


def flash_kernel(info_ref, q_ref, k_ref, v_ref, o_ref, m_ref, l_ref, acc_ref, *, scale, block):
    part = pl.program_id(1)
    last = info_ref[part]
    offset = info_ref[2 + part]
    m_ref[...] = jnp.full(m_ref.shape, NEGATIVE, jnp.float32)
    l_ref[...] = jnp.zeros(l_ref.shape, jnp.float32)
    acc_ref[...] = jnp.zeros(acc_ref.shape, jnp.float32)

    def update(j, masked):
        first = pl.multiple_of(j * block, block)
        scores = lax.dot_general(
            q_ref[0, 0], k_ref[0, pl.ds(first, block), :], (((1,), (1,)), ((), ())),
            preferred_element_type=jnp.float32,
        ) * scale
        if masked:
            rows = lax.broadcasted_iota(jnp.int32, scores.shape, 0) + offset
            cols = lax.broadcasted_iota(jnp.int32, scores.shape, 1)
            scores = jnp.where(cols <= rows, scores, NEGATIVE)
        m_prev = m_ref[:, :1]
        m_new = jnp.maximum(m_prev, jnp.max(scores, axis=1, keepdims=True))
        shrink = jnp.exp(m_prev - m_new)
        weights = jnp.exp(scores - m_new)
        l_new = l_ref[:, :1] * shrink + jnp.sum(weights, axis=1, keepdims=True)
        moved = jnp.dot(
            weights.astype(jnp.bfloat16), v_ref[0, pl.ds(first, block), :],
            preferred_element_type=jnp.float32,
        )
        acc_ref[...] = acc_ref[...] * shrink + moved
        m_ref[...] = jnp.broadcast_to(m_new, m_ref.shape)
        l_ref[...] = jnp.broadcast_to(l_new, l_ref.shape)

    def body(j, carry):
        update(j, False)
        return carry

    lax.fori_loop(0, last, body, 0)
    update(last, True)
    o_ref[0, 0] = (acc_ref[...] / l_ref[:, :1]).astype(o_ref.dtype)


def dense_flash(info, queries, stacked):
    parts, heads, rows, width = queries.shape
    length = stacked.shape[2]
    block = 512
    scale = 1.0 / math.sqrt(width)
    return pl.pallas_call(
        functools.partial(flash_kernel, scale=scale, block=block),
        out_shape=jax.ShapeDtypeStruct((parts, heads, rows, width), jnp.bfloat16),
        grid_spec=pltpu.PrefetchScalarGridSpec(
            num_scalar_prefetch=1,
            grid=(heads, parts),
            in_specs=[
                pl.BlockSpec((1, 1, rows, width), lambda h, p, c: (p, h, 0, 0)),
                pl.BlockSpec((None, 1, length, width), lambda h, p, c: (0, h, 0, 0)),
                pl.BlockSpec((None, 1, length, width), lambda h, p, c: (1, h, 0, 0)),
            ],
            out_specs=pl.BlockSpec((1, 1, rows, width), lambda h, p, c: (p, h, 0, 0)),
            scratch_shapes=[
                pltpu.VMEM((rows, 128), jnp.float32),
                pltpu.VMEM((rows, 128), jnp.float32),
                pltpu.VMEM((rows, width), jnp.float32),
            ],
        ),
        compiler_params=pltpu.CompilerParams(dimension_semantics=("arbitrary", "arbitrary")),
        cost_estimate=pl.CostEstimate(
            flops=2 * parts * heads * rows * length * width,
            transcendentals=parts * heads * rows * length // 2,
            bytes_accessed=stacked.size + 4 * queries.size,
        ),
    )(info, queries, stacked, stacked)


def dense_heads(queries, keys, values):
    tok_rows, heads, width = queries.shape
    count = lax.axis_size("seq")
    me = lax.axis_index("seq").astype(jnp.int32)
    partner = count - 1 - me
    half = tok_rows // 2
    swap = [(i, count - 1 - i) for i in range(count)]
    stacked = jnp.stack([jnp.swapaxes(keys, 0, 1), jnp.swapaxes(values, 0, 1)], axis=0)
    gathered = lax.all_gather(stacked, "seq", axis=2, tiled=True)
    rows_first = jnp.swapaxes(queries, 0, 1)
    lent = lax.ppermute(rows_first[:, half:], "seq", swap)
    both = jnp.stack([rows_first[:, :half], lent], axis=0)
    info = jnp.stack([me, partner, jnp.int32(0), jnp.int32(half)])
    out = dense_flash(info, both, gathered)
    returned = lax.ppermute(out[1], "seq", swap)
    mine = jnp.concatenate([out[0], returned], axis=1)
    return jnp.swapaxes(mine, 0, 1)


def attend_ranked(query_rows, keys, values, gate_rows):
    heads, rows, width = query_rows.shape
    scale = 1.0 / math.sqrt(width)
    ranks = jnp.arange(rows, dtype=jnp.int32)
    scores = jnp.einsum("erd,ekd->erk", query_rows, keys, preferred_element_type=jnp.float32) * scale
    visible = ranks[None, None, :] <= ranks[None, :, None]
    scores = jnp.where(visible, scores, NEGATIVE)
    leading = jnp.max(scores, axis=2, keepdims=True)
    weights = jnp.where(visible, jnp.exp(scores - leading), 0.0)
    total = jnp.sum(weights, axis=2, keepdims=True)
    mixed = (
        jnp.einsum("erk,ekd->erd", weights.astype(jnp.bfloat16), values, preferred_element_type=jnp.float32)
        / total
    )
    return (mixed * jax.nn.sigmoid(gate_rows)[:, :, None]).astype(jnp.bfloat16)


def sparse_heads(queries, keys, values, gate_logit, selection):
    tok_rows, heads, width = queries.shape
    start = lax.axis_index("seq") * tok_rows
    positions = start + jnp.arange(tok_rows, dtype=jnp.int32)
    one_hot = (selection[:, :, None] == positions[None, None, :]).astype(jnp.bfloat16)

    def pick(source):
        return jnp.einsum("ent,ted->end", one_hot, source, preferred_element_type=jnp.float32).astype(
            jnp.bfloat16
        )

    count = lax.axis_size("seq")
    local_kv = jnp.stack([pick(keys), pick(values)], axis=0)
    kinds, heads_, chosen, width_ = local_kv.shape
    pieces = local_kv.reshape(kinds, heads_, count, chosen // count, width_)
    arrived = lax.all_to_all(pieces, "seq", 2, 2, tiled=True)
    own = jnp.sum(arrived.astype(jnp.float32), axis=2).astype(jnp.bfloat16)
    picked_kv = lax.all_gather(own, "seq", axis=2, tiled=True)
    picked_q = pick(queries)
    gate_rows = jnp.einsum("ent,et->en", one_hot, gate_logit, preferred_element_type=jnp.float32)
    results = attend_ranked(picked_q, picked_kv[0], picked_kv[1], gate_rows)
    return jnp.einsum("ent,end->ted", one_hot, results, preferred_element_type=jnp.float32).astype(
        jnp.bfloat16
    )


def local(q_dense, k_dense, v_dense, q_expert, k_expert, v_expert, gate_logit, selection):
    dense_out = dense_heads(q_dense, k_dense, v_dense)
    expert_out = sparse_heads(q_expert, k_expert, v_expert, gate_logit, selection)
    return (dense_out, expert_out)


def solution(mesh):
    rows = P(("dp", "seq"), "head", None)
    placed = (rows, rows, rows, rows, rows, rows, P("head", ("dp", "seq")), P("head", "dp"))
    return jax.shard_map(
        local,
        mesh=mesh,
        in_specs=placed,
        out_specs=(rows, rows),
        check_vma=False,
    )
```

```python
import functools
import math

import jax
import jax.numpy as jnp
from jax import lax
from jax.experimental import pallas as pl
from jax.experimental.pallas import tpu as pltpu
from jax.sharding import PartitionSpec as P

NEGATIVE = -1e30
KEY_BLOCK = 256


def flash_kernel(info_ref, q_ref, k_ref, v_ref, own_ref, lent_ref, *, scale, block):
    part = pl.program_id(1)
    last = info_ref[part]
    offset = info_ref[2 + part]
    rows_n = q_ref.shape[2]

    def update(j, carry, masked):
        m_prev, l_prev, acc = carry
        first = pl.multiple_of(j * block, block)
        scores = lax.dot_general(
            q_ref[0, 0], k_ref[0, pl.ds(first, block), :], (((1,), (1,)), ((), ())),
            preferred_element_type=jnp.float32,
        ) * scale
        if masked:
            rows = lax.broadcasted_iota(jnp.int32, scores.shape, 0) + offset
            cols = lax.broadcasted_iota(jnp.int32, scores.shape, 1)
            scores = jnp.where(cols <= rows, scores, NEGATIVE)
        m_new = jnp.maximum(m_prev, jnp.max(scores, axis=1, keepdims=True))
        shrink = jnp.exp(m_prev - m_new)
        weights = jnp.exp(scores - m_new)
        l_new = l_prev * shrink + jnp.sum(weights, axis=1, keepdims=True)
        moved = jnp.dot(
            weights.astype(jnp.bfloat16), v_ref[0, pl.ds(first, block), :],
            preferred_element_type=jnp.float32,
        )
        return m_new, l_new, acc * shrink + moved

    init = (
        jnp.full((rows_n, 1), NEGATIVE, jnp.float32),
        jnp.zeros((rows_n, 1), jnp.float32),
        jnp.zeros((rows_n, q_ref.shape[3]), jnp.float32),
    )
    carry = lax.fori_loop(0, last, lambda j, c: update(j, c, False), init)
    m_f, l_f, acc_f = update(last, carry, True)
    result = (acc_f / l_f).astype(own_ref.dtype)

    @pl.when(part == 0)
    def _():
        own_ref[0] = result

    @pl.when(part == 1)
    def _():
        lent_ref[0] = result


def dense_flash(info, queries, stacked):
    parts, heads, rows, width = queries.shape
    length = stacked.shape[2]
    block = KEY_BLOCK
    scale = 1.0 / math.sqrt(width)
    return pl.pallas_call(
        functools.partial(flash_kernel, scale=scale, block=block),
        out_shape=[jax.ShapeDtypeStruct((heads, rows, width), jnp.bfloat16)] * 2,
        grid_spec=pltpu.PrefetchScalarGridSpec(
            num_scalar_prefetch=1,
            grid=(heads, parts),
            in_specs=[
                pl.BlockSpec((1, 1, rows, width), lambda h, p, c: (p, h, 0, 0)),
                pl.BlockSpec((None, 1, length, width), lambda h, p, c: (0, h, 0, 0)),
                pl.BlockSpec((None, 1, length, width), lambda h, p, c: (1, h, 0, 0)),
            ],
            out_specs=[pl.BlockSpec((1, rows, width), lambda h, p, c: (h, 0, 0))] * 2,
        ),
        compiler_params=pltpu.CompilerParams(dimension_semantics=("arbitrary", "arbitrary")),
        cost_estimate=pl.CostEstimate(
            flops=2 * parts * heads * rows * length * width,
            transcendentals=parts * heads * rows * length // 2,
            bytes_accessed=stacked.size + 4 * queries.size,
        ),
    )(info, queries, stacked, stacked)


def dense_heads(queries, keys, values):
    tok_rows, heads, width = queries.shape
    count = lax.axis_size("seq")
    me = lax.axis_index("seq").astype(jnp.int32)
    partner = count - 1 - me
    half = tok_rows // 2
    swap = [(i, count - 1 - i) for i in range(count)]
    stacked = jnp.stack([jnp.swapaxes(keys, 0, 1), jnp.swapaxes(values, 0, 1)], axis=0)
    gathered = lax.all_gather(stacked, "seq", axis=2, tiled=True)
    rows_first = jnp.swapaxes(queries, 0, 1)
    lent = lax.ppermute(rows_first[:, half:], "seq", swap)
    both = jnp.stack([rows_first[:, :half], lent], axis=0)
    ends = jnp.stack([me * tok_rows, partner * tok_rows + half])
    lasts = ends // KEY_BLOCK
    info = jnp.concatenate([lasts, ends - lasts * KEY_BLOCK]).astype(jnp.int32)
    ours, theirs = dense_flash(info, both, gathered)
    returned = lax.ppermute(theirs, "seq", swap)
    mine = jnp.concatenate([ours, returned], axis=1)
    return jnp.swapaxes(mine, 0, 1)


def attend_ranked(query_rows, keys, values, gate_rows):
    heads, rows, width = query_rows.shape
    scale = 1.0 / math.sqrt(width)
    ranks = jnp.arange(rows, dtype=jnp.int32)
    scores = jnp.einsum("erd,ekd->erk", query_rows, keys, preferred_element_type=jnp.float32) * scale
    visible = ranks[None, None, :] <= ranks[None, :, None]
    scores = jnp.where(visible, scores, NEGATIVE)
    leading = jnp.max(scores, axis=2, keepdims=True)
    weights = jnp.where(visible, jnp.exp(scores - leading), 0.0)
    total = jnp.sum(weights, axis=2, keepdims=True)
    mixed = (
        jnp.einsum("erk,ekd->erd", weights.astype(jnp.bfloat16), values, preferred_element_type=jnp.float32)
        / total
    )
    return (mixed * jax.nn.sigmoid(gate_rows)[:, :, None]).astype(jnp.bfloat16)


def sparse_heads(queries, keys, values, gate_logit, selection):
    tok_rows, heads, width = queries.shape
    start = lax.axis_index("seq") * tok_rows
    positions = start + jnp.arange(tok_rows, dtype=jnp.int32)
    one_hot = (selection[:, :, None] == positions[None, None, :]).astype(jnp.bfloat16)

    def pick(source):
        return jnp.einsum("ent,ted->end", one_hot, source, preferred_element_type=jnp.float32).astype(
            jnp.bfloat16
        )

    count = lax.axis_size("seq")
    local_kv = jnp.stack([pick(keys), pick(values)], axis=0)
    kinds, heads_, chosen, width_ = local_kv.shape
    pieces = local_kv.reshape(kinds, heads_, count, chosen // count, width_)
    arrived = lax.all_to_all(pieces, "seq", 2, 2, tiled=True)
    own = jnp.sum(arrived.astype(jnp.float32), axis=2).astype(jnp.bfloat16)
    picked_kv = lax.all_gather(own, "seq", axis=2, tiled=True)
    picked_q = pick(queries)
    gate_rows = jnp.einsum("ent,et->en", one_hot, gate_logit, preferred_element_type=jnp.float32)
    results = attend_ranked(picked_q, picked_kv[0], picked_kv[1], gate_rows)
    return jnp.einsum("ent,end->ted", one_hot, results, preferred_element_type=jnp.float32).astype(
        jnp.bfloat16
    )


def local(q_dense, k_dense, v_dense, q_expert, k_expert, v_expert, gate_logit, selection):
    dense_out = dense_heads(q_dense, k_dense, v_dense)
    expert_out = sparse_heads(q_expert, k_expert, v_expert, gate_logit, selection)
    return (dense_out, expert_out)


def solution(mesh):
    rows = P(("dp", "seq"), "head", None)
    placed = (rows, rows, rows, rows, rows, rows, P("head", ("dp", "seq")), P("head", "dp"))
    return jax.shard_map(
        local,
        mesh=mesh,
        in_specs=placed,
        out_specs=(rows, rows),
        check_vma=False,
    )
```

```python
import functools
import math

import jax
import jax.numpy as jnp
from jax import lax
from jax.experimental import pallas as pl
from jax.experimental.pallas import tpu as pltpu
from jax.sharding import PartitionSpec as P

NEGATIVE = -1e30
KEY_BLOCK = 512


def flash_kernel(info_ref, q_ref, k_ref, v_ref, own_ref, lent_ref, *, scale, block):
    part = pl.program_id(1)
    last = info_ref[part]
    offset = info_ref[2 + part]
    rows_n = q_ref.shape[2]

    def update(j, carry, masked):
        m_prev, l_prev, acc = carry
        first = pl.multiple_of(j * block, block)
        scores = lax.dot_general(
            q_ref[0, 0], k_ref[0, pl.ds(first, block), :], (((1,), (1,)), ((), ())),
            preferred_element_type=jnp.float32,
        ) * scale
        if masked:
            rows = lax.broadcasted_iota(jnp.int32, scores.shape, 0) + offset
            cols = lax.broadcasted_iota(jnp.int32, scores.shape, 1)
            scores = jnp.where(cols <= rows, scores, NEGATIVE)
        m_new = jnp.maximum(m_prev, jnp.max(scores, axis=1, keepdims=True))
        shrink = jnp.exp(m_prev - m_new)
        weights = jnp.exp(scores - m_new)
        l_new = l_prev * shrink + jnp.sum(weights, axis=1, keepdims=True)
        moved = jnp.dot(
            weights.astype(jnp.bfloat16), v_ref[0, pl.ds(first, block), :],
            preferred_element_type=jnp.float32,
        )
        return m_new, l_new, acc * shrink + moved

    init = (
        jnp.full((rows_n, 1), NEGATIVE, jnp.float32),
        jnp.zeros((rows_n, 1), jnp.float32),
        jnp.zeros((rows_n, q_ref.shape[3]), jnp.float32),
    )
    carry = lax.fori_loop(0, last, lambda j, c: update(j, c, False), init)
    m_f, l_f, acc_f = update(last, carry, True)
    result = (acc_f / l_f).astype(own_ref.dtype)

    @pl.when(part == 0)
    def _():
        own_ref[0] = result

    @pl.when(part == 1)
    def _():
        lent_ref[0] = result


def dense_flash(info, queries, stacked):
    parts, heads, rows, width = queries.shape
    length = stacked.shape[2]
    block = KEY_BLOCK
    scale = 1.0 / math.sqrt(width)
    return pl.pallas_call(
        functools.partial(flash_kernel, scale=scale, block=block),
        out_shape=[jax.ShapeDtypeStruct((heads, rows, width), jnp.bfloat16)] * 2,
        grid_spec=pltpu.PrefetchScalarGridSpec(
            num_scalar_prefetch=1,
            grid=(heads, parts),
            in_specs=[
                pl.BlockSpec((1, 1, rows, width), lambda h, p, c: (p, h, 0, 0)),
                pl.BlockSpec((None, 1, length, width), lambda h, p, c: (0, h, 0, 0)),
                pl.BlockSpec((None, 1, length, width), lambda h, p, c: (1, h, 0, 0)),
            ],
            out_specs=[pl.BlockSpec((1, rows, width), lambda h, p, c: (h, 0, 0))] * 2,
        ),
        compiler_params=pltpu.CompilerParams(dimension_semantics=("arbitrary", "arbitrary")),
        cost_estimate=pl.CostEstimate(
            flops=2 * parts * heads * rows * length * width,
            transcendentals=parts * heads * rows * length // 2,
            bytes_accessed=stacked.size + 4 * queries.size,
        ),
    )(info, queries, stacked, stacked)


def dense_heads(queries, keys, values):
    tok_rows, heads, width = queries.shape
    count = lax.axis_size("seq")
    me = lax.axis_index("seq").astype(jnp.int32)
    partner = count - 1 - me
    half = tok_rows // 2
    swap = [(i, count - 1 - i) for i in range(count)]
    stacked = jnp.stack([jnp.swapaxes(keys, 0, 1), jnp.swapaxes(values, 0, 1)], axis=0)
    gathered = lax.all_gather(stacked, "seq", axis=2, tiled=True)
    rows_first = jnp.swapaxes(queries, 0, 1)
    lent = lax.ppermute(rows_first[:, half:], "seq", swap)
    both = jnp.stack([rows_first[:, :half], lent], axis=0)
    ends = jnp.stack([me * tok_rows, partner * tok_rows + half])
    lasts = ends // KEY_BLOCK
    info = jnp.concatenate([lasts, ends - lasts * KEY_BLOCK]).astype(jnp.int32)
    ours, theirs = dense_flash(info, both, gathered)
    returned = lax.ppermute(theirs, "seq", swap)
    mine = jnp.concatenate([ours, returned], axis=1)
    return jnp.swapaxes(mine, 0, 1)


def attend_ranked(query_rows, keys, values, gate_rows):
    heads, rows, width = query_rows.shape
    scale = 1.0 / math.sqrt(width)
    ranks = jnp.arange(rows, dtype=jnp.int32)
    scores = jnp.einsum("erd,ekd->erk", query_rows, keys, preferred_element_type=jnp.float32) * scale
    visible = ranks[None, None, :] <= ranks[None, :, None]
    scores = jnp.where(visible, scores, NEGATIVE)
    leading = jnp.max(scores, axis=2, keepdims=True)
    weights = jnp.where(visible, jnp.exp(scores - leading), 0.0)
    total = jnp.sum(weights, axis=2, keepdims=True)
    mixed = (
        jnp.einsum("erk,ekd->erd", weights.astype(jnp.bfloat16), values, preferred_element_type=jnp.float32)
        / total
    )
    return (mixed * jax.nn.sigmoid(gate_rows)[:, :, None]).astype(jnp.bfloat16)


def sparse_heads(queries, keys, values, gate_logit, selection):
    tok_rows, heads, width = queries.shape
    start = lax.axis_index("seq") * tok_rows
    positions = start + jnp.arange(tok_rows, dtype=jnp.int32)
    one_hot = (selection[:, :, None] == positions[None, None, :]).astype(jnp.bfloat16)

    def pick(source):
        return jnp.einsum("ent,ted->end", one_hot, source, preferred_element_type=jnp.float32).astype(
            jnp.bfloat16
        )

    count = lax.axis_size("seq")
    local_kv = jnp.stack([pick(keys), pick(values)], axis=0)
    kinds, heads_, chosen, width_ = local_kv.shape
    pieces = local_kv.reshape(kinds, heads_, count, chosen // count, width_)
    arrived = lax.all_to_all(pieces, "seq", 2, 2, tiled=True)
    own = jnp.sum(arrived.astype(jnp.float32), axis=2).astype(jnp.bfloat16)
    picked_kv = lax.all_gather(own, "seq", axis=2, tiled=True)
    picked_q = pick(queries)
    gate_rows = jnp.einsum("ent,et->en", one_hot, gate_logit, preferred_element_type=jnp.float32)
    results = attend_ranked(picked_q, picked_kv[0], picked_kv[1], gate_rows)
    return jnp.einsum("ent,end->ted", one_hot, results, preferred_element_type=jnp.float32).astype(
        jnp.bfloat16
    )


def local(q_dense, k_dense, v_dense, q_expert, k_expert, v_expert, gate_logit, selection):
    dense_out = dense_heads(q_dense, k_dense, v_dense)
    expert_out = sparse_heads(q_expert, k_expert, v_expert, gate_logit, selection)
    return (dense_out, expert_out)


def solution(mesh):
    rows = P(("dp", "seq"), "head", None)
    placed = (rows, rows, rows, rows, rows, rows, P("head", ("dp", "seq")), P("head", "dp"))
    return jax.shard_map(
        local,
        mesh=mesh,
        in_specs=placed,
        out_specs=(rows, rows),
        check_vma=False,
    )
```

```python
import functools
import math

import jax
import jax.numpy as jnp
from jax import lax
from jax.experimental import pallas as pl
from jax.experimental.pallas import tpu as pltpu
from jax.sharding import PartitionSpec as P

NEGATIVE = -1e30
KEY_BLOCK = 512


def flash_kernel(info_ref, q_ref, k_ref, v_ref, own_ref, lent_ref, *, scale, block):
    part = pl.program_id(1)
    last = info_ref[part]
    offset = info_ref[2 + part]
    rows_n = q_ref.shape[2]

    def update(j, carry, masked):
        m_prev, l_prev, acc = carry
        first = pl.multiple_of(j * block, block)
        scores = lax.dot_general(
            q_ref[0, 0], k_ref[0, pl.ds(first, block), :], (((1,), (1,)), ((), ())),
            preferred_element_type=jnp.float32,
        ) * scale
        if masked:
            rows = lax.broadcasted_iota(jnp.int32, scores.shape, 0) + offset
            cols = lax.broadcasted_iota(jnp.int32, scores.shape, 1)
            scores = jnp.where(cols <= rows, scores, NEGATIVE)
        m_new = jnp.maximum(m_prev, jnp.max(scores, axis=1, keepdims=True))
        shrink = jnp.exp(m_prev - m_new)
        weights = jnp.exp(scores - m_new)
        l_new = l_prev * shrink + jnp.sum(weights, axis=1, keepdims=True)
        moved = jnp.dot(
            weights.astype(jnp.bfloat16), v_ref[0, pl.ds(first, block), :],
            preferred_element_type=jnp.float32,
        )
        return m_new, l_new, acc * shrink + moved

    init = (
        jnp.full((rows_n, 1), NEGATIVE, jnp.float32),
        jnp.zeros((rows_n, 1), jnp.float32),
        jnp.zeros((rows_n, q_ref.shape[3]), jnp.float32),
    )
    carry = lax.fori_loop(0, last, lambda j, c: update(j, c, False), init)
    m_f, l_f, acc_f = update(last, carry, True)
    result = (acc_f / l_f).astype(own_ref.dtype)

    @pl.when(part == 0)
    def _():
        own_ref[0] = result

    @pl.when(part == 1)
    def _():
        lent_ref[0] = result


def dense_flash(info, queries, stacked):
    parts, heads, rows, width = queries.shape
    length = stacked.shape[2]
    block = KEY_BLOCK
    scale = 1.0 / math.sqrt(width)
    return pl.pallas_call(
        functools.partial(flash_kernel, scale=scale, block=block),
        out_shape=[jax.ShapeDtypeStruct((heads, rows, width), jnp.bfloat16)] * 2,
        grid_spec=pltpu.PrefetchScalarGridSpec(
            num_scalar_prefetch=1,
            grid=(heads, parts),
            in_specs=[
                pl.BlockSpec((1, 1, rows, width), lambda h, p, c: (p, h, 0, 0)),
                pl.BlockSpec((None, 1, length, width), lambda h, p, c: (0, h, 0, 0)),
                pl.BlockSpec((None, 1, length, width), lambda h, p, c: (1, h, 0, 0)),
            ],
            out_specs=[pl.BlockSpec((1, rows, width), lambda h, p, c: (h, 0, 0))] * 2,
        ),
        compiler_params=pltpu.CompilerParams(dimension_semantics=("arbitrary", "arbitrary")),
        cost_estimate=pl.CostEstimate(
            flops=2 * parts * heads * rows * length * width,
            transcendentals=parts * heads * rows * length // 2,
            bytes_accessed=stacked.size + 4 * queries.size,
        ),
    )(info, queries, stacked, stacked)


def dense_heads(queries, keys, values):
    tok_rows, heads, width = queries.shape
    count = lax.axis_size("seq")
    me = lax.axis_index("seq").astype(jnp.int32)
    partner = count - 1 - me
    half = tok_rows // 2
    swap = [(i, count - 1 - i) for i in range(count)]
    stacked = jnp.stack([jnp.swapaxes(keys, 0, 1), jnp.swapaxes(values, 0, 1)], axis=0)
    gathered = lax.all_gather(stacked, "seq", axis=2, tiled=True)
    rows_first = jnp.swapaxes(queries, 0, 1)
    lent = lax.ppermute(rows_first[:, half:], "seq", swap)
    both = jnp.stack([rows_first[:, :half], lent], axis=0)
    ends = jnp.stack([me * tok_rows, partner * tok_rows + half])
    lasts = ends // KEY_BLOCK
    info = jnp.concatenate([lasts, ends - lasts * KEY_BLOCK]).astype(jnp.int32)
    ours, theirs = dense_flash(info, both, gathered)
    returned = lax.ppermute(theirs, "seq", swap)
    mine = jnp.concatenate([ours, returned], axis=1)
    return jnp.swapaxes(mine, 0, 1)


def attend_ranked(query_rows, keys, values, gate_rows):
    heads, rows, width = query_rows.shape
    scale = 1.0 / math.sqrt(width)
    ranks = jnp.arange(rows, dtype=jnp.int32)
    scores = jnp.einsum("erd,ekd->erk", query_rows, keys, preferred_element_type=jnp.float32) * scale
    visible = ranks[None, None, :] <= ranks[None, :, None]
    scores = jnp.where(visible, scores, NEGATIVE)
    leading = jnp.max(scores, axis=2, keepdims=True)
    weights = jnp.where(visible, jnp.exp(scores - leading), 0.0)
    total = jnp.sum(weights, axis=2, keepdims=True)
    mixed = (
        jnp.einsum("erk,ekd->erd", weights.astype(jnp.bfloat16), values, preferred_element_type=jnp.float32)
        / total
    )
    return (mixed * jax.nn.sigmoid(gate_rows)[:, :, None]).astype(jnp.bfloat16)


def sparse_heads(queries, keys, values, gate_logit, selection):
    tok_rows, heads, width = queries.shape
    start = lax.axis_index("seq") * tok_rows
    positions = start + jnp.arange(tok_rows, dtype=jnp.int32)
    one_hot = (selection[:, :, None] == positions[None, None, :]).astype(jnp.bfloat16)

    def pick(source):
        return jnp.einsum("ent,ted->end", one_hot, source, preferred_element_type=jnp.float32).astype(
            jnp.bfloat16
        )

    count = lax.axis_size("seq")
    local_kv = jnp.stack([pick(keys), pick(values)], axis=0)
    kinds, heads_, chosen, width_ = local_kv.shape
    pieces = local_kv.reshape(kinds, heads_, count, chosen // count, width_)
    arrived = lax.all_to_all(pieces, "seq", 2, 2, tiled=True)
    own = jnp.sum(arrived.astype(jnp.float32), axis=2).astype(jnp.bfloat16)
    spread = jnp.broadcast_to(own[:, :, None], (kinds, heads_, count) + own.shape[2:])
    picked_kv = lax.all_to_all(spread, "seq", 2, 2, tiled=True).reshape(kinds, heads_, chosen, width_)
    picked_q = pick(queries)
    gate_rows = jnp.einsum("ent,et->en", one_hot, gate_logit, preferred_element_type=jnp.float32)
    results = attend_ranked(picked_q, picked_kv[0], picked_kv[1], gate_rows)
    return jnp.einsum("ent,end->ted", one_hot, results, preferred_element_type=jnp.float32).astype(
        jnp.bfloat16
    )


def local(q_dense, k_dense, v_dense, q_expert, k_expert, v_expert, gate_logit, selection):
    dense_out = dense_heads(q_dense, k_dense, v_dense)
    expert_out = sparse_heads(q_expert, k_expert, v_expert, gate_logit, selection)
    return (dense_out, expert_out)


def solution(mesh):
    rows = P(("dp", "seq"), "head", None)
    placed = (rows, rows, rows, rows, rows, rows, P("head", ("dp", "seq")), P("head", "dp"))
    return jax.shard_map(
        local,
        mesh=mesh,
        in_specs=placed,
        out_specs=(rows, rows),
        check_vma=False,
    )
```

```python
import functools
import math

import jax
import jax.numpy as jnp
from jax import lax
from jax.experimental import pallas as pl
from jax.experimental.pallas import tpu as pltpu
from jax.sharding import PartitionSpec as P

NEGATIVE = -1e30
KEY_BLOCK = 2048


def flash_kernel(info_ref, q_ref, k_ref, v_ref, own_ref, lent_ref, *, scale, block):
    part = pl.program_id(1)
    last = info_ref[part]
    offset = info_ref[2 + part]
    rows_n = q_ref.shape[2]

    def update(j, carry, masked):
        m_prev, l_prev, acc = carry
        first = pl.multiple_of(j * block, block)
        scores = lax.dot_general(
            q_ref[0, 0], k_ref[0, pl.ds(first, block), :], (((1,), (1,)), ((), ())),
            preferred_element_type=jnp.float32,
        ) * scale
        if masked:
            rows = lax.broadcasted_iota(jnp.int32, scores.shape, 0) + offset
            cols = lax.broadcasted_iota(jnp.int32, scores.shape, 1)
            scores = jnp.where(cols <= rows, scores, NEGATIVE)
        m_new = jnp.maximum(m_prev, jnp.max(scores, axis=1, keepdims=True))
        shrink = jnp.exp(m_prev - m_new)
        weights = jnp.exp(scores - m_new)
        l_new = l_prev * shrink + jnp.sum(weights, axis=1, keepdims=True)
        moved = jnp.dot(
            weights.astype(jnp.bfloat16), v_ref[0, pl.ds(first, block), :],
            preferred_element_type=jnp.float32,
        )
        return m_new, l_new, acc * shrink + moved

    init = (
        jnp.full((rows_n, 1), NEGATIVE, jnp.float32),
        jnp.zeros((rows_n, 1), jnp.float32),
        jnp.zeros((rows_n, q_ref.shape[3]), jnp.float32),
    )
    carry = lax.fori_loop(0, last, lambda j, c: update(j, c, False), init)
    m_f, l_f, acc_f = update(last, carry, True)
    result = (acc_f / l_f).astype(own_ref.dtype)

    @pl.when(part == 0)
    def _():
        own_ref[0] = result

    @pl.when(part == 1)
    def _():
        lent_ref[0] = result


def dense_flash(info, queries, stacked):
    parts, heads, rows, width = queries.shape
    length = stacked.shape[2]
    block = KEY_BLOCK
    scale = 1.0 / math.sqrt(width)
    return pl.pallas_call(
        functools.partial(flash_kernel, scale=scale, block=block),
        out_shape=[jax.ShapeDtypeStruct((heads, rows, width), jnp.bfloat16)] * 2,
        grid_spec=pltpu.PrefetchScalarGridSpec(
            num_scalar_prefetch=1,
            grid=(heads, parts),
            in_specs=[
                pl.BlockSpec((1, 1, rows, width), lambda h, p, c: (p, h, 0, 0)),
                pl.BlockSpec((None, 1, length, width), lambda h, p, c: (0, h, 0, 0)),
                pl.BlockSpec((None, 1, length, width), lambda h, p, c: (1, h, 0, 0)),
            ],
            out_specs=[pl.BlockSpec((1, rows, width), lambda h, p, c: (h, 0, 0))] * 2,
        ),
        compiler_params=pltpu.CompilerParams(dimension_semantics=("arbitrary", "arbitrary")),
        cost_estimate=pl.CostEstimate(
            flops=2 * parts * heads * rows * length * width,
            transcendentals=parts * heads * rows * length // 2,
            bytes_accessed=stacked.size + 4 * queries.size,
        ),
    )(info, queries, stacked, stacked)


def dense_heads(queries, keys, values):
    tok_rows, heads, width = queries.shape
    count = lax.axis_size("seq")
    me = lax.axis_index("seq").astype(jnp.int32)
    partner = count - 1 - me
    half = tok_rows // 2
    swap = [(i, count - 1 - i) for i in range(count)]
    stacked = jnp.stack([jnp.swapaxes(keys, 0, 1), jnp.swapaxes(values, 0, 1)], axis=0)
    gathered = lax.all_gather(stacked, "seq", axis=2, tiled=True)
    rows_first = jnp.swapaxes(queries, 0, 1)
    lent = lax.ppermute(rows_first[:, half:], "seq", swap)
    both = jnp.stack([rows_first[:, :half], lent], axis=0)
    ends = jnp.stack([me * tok_rows, partner * tok_rows + half])
    lasts = (ends + half - 1) // KEY_BLOCK
    info = jnp.concatenate([lasts, ends - lasts * KEY_BLOCK]).astype(jnp.int32)
    ours, theirs = dense_flash(info, both, gathered)
    returned = lax.ppermute(theirs, "seq", swap)
    mine = jnp.concatenate([ours, returned], axis=1)
    return jnp.swapaxes(mine, 0, 1)


def attend_ranked(query_rows, keys, values, gate_rows):
    heads, rows, width = query_rows.shape
    scale = 1.0 / math.sqrt(width)
    ranks = jnp.arange(rows, dtype=jnp.int32)
    scores = jnp.einsum("erd,ekd->erk", query_rows, keys, preferred_element_type=jnp.float32) * scale
    visible = ranks[None, None, :] <= ranks[None, :, None]
    scores = jnp.where(visible, scores, NEGATIVE)
    leading = jnp.max(scores, axis=2, keepdims=True)
    weights = jnp.where(visible, jnp.exp(scores - leading), 0.0)
    total = jnp.sum(weights, axis=2, keepdims=True)
    mixed = (
        jnp.einsum("erk,ekd->erd", weights.astype(jnp.bfloat16), values, preferred_element_type=jnp.float32)
        / total
    )
    return (mixed * jax.nn.sigmoid(gate_rows)[:, :, None]).astype(jnp.bfloat16)


def sparse_heads(queries, keys, values, gate_logit, selection):
    tok_rows, heads, width = queries.shape
    start = lax.axis_index("seq") * tok_rows
    positions = start + jnp.arange(tok_rows, dtype=jnp.int32)
    one_hot = (selection[:, :, None] == positions[None, None, :]).astype(jnp.bfloat16)

    def pick(source):
        return jnp.einsum("ent,ted->end", one_hot, source, preferred_element_type=jnp.float32).astype(
            jnp.bfloat16
        )

    count = lax.axis_size("seq")
    local_kv = jnp.stack([pick(keys), pick(values)], axis=0)
    kinds, heads_, chosen, width_ = local_kv.shape
    pieces = local_kv.reshape(kinds, heads_, count, chosen // count, width_)
    arrived = lax.all_to_all(pieces, "seq", 2, 2, tiled=True)
    own = jnp.sum(arrived.astype(jnp.float32), axis=2).astype(jnp.bfloat16)
    picked_kv = lax.all_gather(own, "seq", axis=2, tiled=True)
    picked_q = pick(queries)
    gate_rows = jnp.einsum("ent,et->en", one_hot, gate_logit, preferred_element_type=jnp.float32)
    results = attend_ranked(picked_q, picked_kv[0], picked_kv[1], gate_rows)
    return jnp.einsum("ent,end->ted", one_hot, results, preferred_element_type=jnp.float32).astype(
        jnp.bfloat16
    )


def local(q_dense, k_dense, v_dense, q_expert, k_expert, v_expert, gate_logit, selection):
    dense_out = dense_heads(q_dense, k_dense, v_dense)
    expert_out = sparse_heads(q_expert, k_expert, v_expert, gate_logit, selection)
    return (dense_out, expert_out)


def solution(mesh):
    rows = P(("dp", "seq"), "head", None)
    placed = (rows, rows, rows, rows, rows, rows, P("head", ("dp", "seq")), P("head", "dp"))
    return jax.shard_map(
        local,
        mesh=mesh,
        in_specs=placed,
        out_specs=(rows, rows),
        check_vma=False,
    )
```

```python
import functools
import math

import jax
import jax.numpy as jnp
from jax import lax
from jax.experimental import pallas as pl
from jax.experimental.pallas import tpu as pltpu
from jax.sharding import PartitionSpec as P

NEGATIVE = -1e30
KEY_BLOCK = 2048


def flash_kernel(info_ref, q_ref, k_ref, v_ref, own_ref, lent_ref, *, scale, block):
    part = pl.program_id(1)
    last = info_ref[part]
    offset = info_ref[2 + part]
    rows_n = q_ref.shape[2]

    def update(j, carry, masked):
        m_prev, l_prev, acc = carry
        first = pl.multiple_of(j * block, block)
        scores = lax.dot_general(
            q_ref[0, 0], k_ref[0, pl.ds(first, block), :], (((1,), (1,)), ((), ())),
            preferred_element_type=jnp.float32,
        ) * scale
        if masked:
            rows = lax.broadcasted_iota(jnp.int32, scores.shape, 0) + offset
            cols = lax.broadcasted_iota(jnp.int32, scores.shape, 1)
            scores = jnp.where(cols <= rows, scores, NEGATIVE)
        m_new = jnp.maximum(m_prev, jnp.max(scores, axis=1, keepdims=True))
        shrink = jnp.exp(m_prev - m_new)
        weights = jnp.exp(scores - m_new)
        l_new = l_prev * shrink + jnp.sum(weights, axis=1, keepdims=True)
        moved = jnp.dot(
            weights.astype(jnp.bfloat16), v_ref[0, pl.ds(first, block), :],
            preferred_element_type=jnp.float32,
        )
        return m_new, l_new, acc * shrink + moved

    init = (
        jnp.full((rows_n, 1), NEGATIVE, jnp.float32),
        jnp.zeros((rows_n, 1), jnp.float32),
        jnp.zeros((rows_n, q_ref.shape[3]), jnp.float32),
    )
    carry = lax.fori_loop(0, last, lambda j, c: update(j, c, False), init)
    m_f, l_f, acc_f = update(last, carry, True)
    result = (acc_f / l_f).astype(own_ref.dtype)

    @pl.when(part == 0)
    def _():
        own_ref[0] = result

    @pl.when(part == 1)
    def _():
        lent_ref[0] = result


def dense_flash(info, queries, stacked, head=0):
    parts, heads, rows, width = queries.shape
    length = stacked.shape[2]
    block = KEY_BLOCK
    scale = 1.0 / math.sqrt(width)
    return pl.pallas_call(
        functools.partial(flash_kernel, scale=scale, block=block),
        out_shape=[jax.ShapeDtypeStruct((heads, rows, width), jnp.bfloat16)] * 2,
        grid_spec=pltpu.PrefetchScalarGridSpec(
            num_scalar_prefetch=1,
            grid=(heads, parts),
            in_specs=[
                pl.BlockSpec((1, 1, rows, width), lambda h, p, c: (p, h, 0, 0)),
                pl.BlockSpec((None, 1, length, width), lambda h, p, c: (0, h + head, 0, 0)),
                pl.BlockSpec((None, 1, length, width), lambda h, p, c: (1, h + head, 0, 0)),
            ],
            out_specs=[pl.BlockSpec((1, rows, width), lambda h, p, c: (h, 0, 0))] * 2,
        ),
        compiler_params=pltpu.CompilerParams(dimension_semantics=("arbitrary", "arbitrary")),
        cost_estimate=pl.CostEstimate(
            flops=2 * parts * heads * rows * length * width,
            transcendentals=parts * heads * rows * length // 2,
            bytes_accessed=stacked.size + 4 * queries.size,
        ),
    )(info, queries, stacked, stacked)


def dense_heads(queries, keys, values):
    tok_rows, heads, width = queries.shape
    count = lax.axis_size("seq")
    me = lax.axis_index("seq").astype(jnp.int32)
    partner = count - 1 - me
    half = tok_rows // 2
    swap = [(i, count - 1 - i) for i in range(count)]
    stacked = jnp.stack([jnp.swapaxes(keys, 0, 1), jnp.swapaxes(values, 0, 1)], axis=0)
    gathered = lax.all_gather(stacked, "seq", axis=2, tiled=True)
    rows_first = jnp.swapaxes(queries, 0, 1)
    lent = lax.ppermute(rows_first[:, half:], "seq", swap)
    both = jnp.stack([rows_first[:, :half], lent], axis=0)
    ends = jnp.stack([me * tok_rows, partner * tok_rows + half])
    lasts = (ends + half - 1) // KEY_BLOCK
    info = jnp.concatenate([lasts, ends - lasts * KEY_BLOCK]).astype(jnp.int32)
    pieces = []
    for h in range(heads):
        ours, theirs = dense_flash(info, both[:, h : h + 1], gathered, h)
        pieces.append(jnp.concatenate([ours, lax.ppermute(theirs, "seq", swap)], axis=1))
    mine = jnp.concatenate(pieces, axis=0)
    return jnp.swapaxes(mine, 0, 1)


def attend_ranked(query_rows, keys, values, gate_rows):
    heads, rows, width = query_rows.shape
    scale = 1.0 / math.sqrt(width)
    ranks = jnp.arange(rows, dtype=jnp.int32)
    scores = jnp.einsum("erd,ekd->erk", query_rows, keys, preferred_element_type=jnp.float32) * scale
    visible = ranks[None, None, :] <= ranks[None, :, None]
    scores = jnp.where(visible, scores, NEGATIVE)
    leading = jnp.max(scores, axis=2, keepdims=True)
    weights = jnp.where(visible, jnp.exp(scores - leading), 0.0)
    total = jnp.sum(weights, axis=2, keepdims=True)
    mixed = (
        jnp.einsum("erk,ekd->erd", weights.astype(jnp.bfloat16), values, preferred_element_type=jnp.float32)
        / total
    )
    return (mixed * jax.nn.sigmoid(gate_rows)[:, :, None]).astype(jnp.bfloat16)


def sparse_heads(queries, keys, values, gate_logit, selection):
    tok_rows, heads, width = queries.shape
    start = lax.axis_index("seq") * tok_rows
    positions = start + jnp.arange(tok_rows, dtype=jnp.int32)
    one_hot = (selection[:, :, None] == positions[None, None, :]).astype(jnp.bfloat16)

    def pick(source):
        return jnp.einsum("ent,ted->end", one_hot, source, preferred_element_type=jnp.float32).astype(
            jnp.bfloat16
        )

    count = lax.axis_size("seq")
    local_kv = jnp.stack([pick(keys), pick(values)], axis=0)
    kinds, heads_, chosen, width_ = local_kv.shape
    pieces = local_kv.reshape(kinds, heads_, count, chosen // count, width_)
    arrived = lax.all_to_all(pieces, "seq", 2, 2, tiled=True)
    own = jnp.sum(arrived.astype(jnp.float32), axis=2).astype(jnp.bfloat16)
    picked_kv = lax.all_gather(own, "seq", axis=2, tiled=True)
    picked_q = pick(queries)
    gate_rows = jnp.einsum("ent,et->en", one_hot, gate_logit, preferred_element_type=jnp.float32)
    results = attend_ranked(picked_q, picked_kv[0], picked_kv[1], gate_rows)
    return jnp.einsum("ent,end->ted", one_hot, results, preferred_element_type=jnp.float32).astype(
        jnp.bfloat16
    )


def local(q_dense, k_dense, v_dense, q_expert, k_expert, v_expert, gate_logit, selection):
    dense_out = dense_heads(q_dense, k_dense, v_dense)
    expert_out = sparse_heads(q_expert, k_expert, v_expert, gate_logit, selection)
    return (dense_out, expert_out)


def solution(mesh):
    rows = P(("dp", "seq"), "head", None)
    placed = (rows, rows, rows, rows, rows, rows, P("head", ("dp", "seq")), P("head", "dp"))
    return jax.shard_map(
        local,
        mesh=mesh,
        in_specs=placed,
        out_specs=(rows, rows),
        check_vma=False,
    )
```

```python
import functools
import math

import jax
import jax.numpy as jnp
from jax import lax
from jax.experimental import pallas as pl
from jax.experimental.pallas import tpu as pltpu
from jax.sharding import PartitionSpec as P

NEGATIVE = -1e30
KEY_BLOCK = 2048


def flash_kernel(info_ref, q_ref, k_ref, v_ref, own_ref, lent_ref, *, scale, block):
    part = pl.program_id(1)
    last = info_ref[part]
    offset = info_ref[2 + part]
    rows_n = q_ref.shape[2]

    def update(j, carry, masked):
        m_prev, l_prev, acc = carry
        per = block // k_ref.shape[1]
        first = pl.multiple_of(j * per, per)
        keys = k_ref[pl.ds(first, per)].reshape(block, k_ref.shape[2])
        scores = lax.dot_general(
            q_ref[0, 0], keys, (((1,), (1,)), ((), ())),
            preferred_element_type=jnp.float32,
        ) * scale
        if masked:
            rows = lax.broadcasted_iota(jnp.int32, scores.shape, 0) + offset
            cols = lax.broadcasted_iota(jnp.int32, scores.shape, 1)
            scores = jnp.where(cols <= rows, scores, NEGATIVE)
        m_new = jnp.maximum(m_prev, jnp.max(scores, axis=1, keepdims=True))
        shrink = jnp.exp(m_prev - m_new)
        weights = jnp.exp(scores - m_new)
        l_new = l_prev * shrink + jnp.sum(weights, axis=1, keepdims=True)
        moved = jnp.dot(
            weights.astype(jnp.bfloat16), v_ref[pl.ds(first, per)].reshape(block, v_ref.shape[2]),
            preferred_element_type=jnp.float32,
        )
        return m_new, l_new, acc * shrink + moved

    init = (
        jnp.full((rows_n, 1), NEGATIVE, jnp.float32),
        jnp.zeros((rows_n, 1), jnp.float32),
        jnp.zeros((rows_n, q_ref.shape[3]), jnp.float32),
    )
    carry = lax.fori_loop(0, last, lambda j, c: update(j, c, False), init)
    m_f, l_f, acc_f = update(last, carry, True)
    result = (acc_f / l_f).astype(own_ref.dtype)

    @pl.when(part == 0)
    def _():
        own_ref[0] = result

    @pl.when(part == 1)
    def _():
        lent_ref[0] = result


def dense_flash(info, queries, stacked):
    parts, heads, rows, width = queries.shape
    pieces, kinds, heads_kv, sub, width_kv = stacked.shape
    length = pieces * sub
    block = KEY_BLOCK
    scale = 1.0 / math.sqrt(width)
    return pl.pallas_call(
        functools.partial(flash_kernel, scale=scale, block=block),
        out_shape=[jax.ShapeDtypeStruct((heads, rows, width), jnp.bfloat16)] * 2,
        grid_spec=pltpu.PrefetchScalarGridSpec(
            num_scalar_prefetch=1,
            grid=(heads, parts),
            in_specs=[
                pl.BlockSpec((1, 1, rows, width), lambda h, p, c: (p, h, 0, 0)),
                pl.BlockSpec((pieces, None, None, sub, width), lambda h, p, c: (0, 0, h, 0, 0)),
                pl.BlockSpec((pieces, None, None, sub, width), lambda h, p, c: (0, 1, h, 0, 0)),
            ],
            out_specs=[pl.BlockSpec((1, rows, width), lambda h, p, c: (h, 0, 0))] * 2,
        ),
        compiler_params=pltpu.CompilerParams(dimension_semantics=("arbitrary", "arbitrary")),
        cost_estimate=pl.CostEstimate(
            flops=2 * parts * heads * rows * length * width,
            transcendentals=parts * heads * rows * length // 2,
            bytes_accessed=stacked.size + 4 * queries.size,
        ),
    )(info, queries, stacked, stacked)


def dense_heads(queries, keys, values):
    tok_rows, heads, width = queries.shape
    count = lax.axis_size("seq")
    me = lax.axis_index("seq").astype(jnp.int32)
    partner = count - 1 - me
    half = tok_rows // 2
    swap = [(i, count - 1 - i) for i in range(count)]
    stacked = jnp.stack([jnp.swapaxes(keys, 0, 1), jnp.swapaxes(values, 0, 1)], axis=0)
    gathered = lax.all_gather(stacked, "seq", axis=0)
    rows_first = jnp.swapaxes(queries, 0, 1)
    lent = lax.ppermute(rows_first[:, half:], "seq", swap)
    both = jnp.stack([rows_first[:, :half], lent], axis=0)
    ends = jnp.stack([me * tok_rows, partner * tok_rows + half])
    lasts = (ends + half - 1) // KEY_BLOCK
    info = jnp.concatenate([lasts, ends - lasts * KEY_BLOCK]).astype(jnp.int32)
    ours, theirs = dense_flash(info, both, gathered)
    returned = lax.ppermute(theirs, "seq", swap)
    mine = jnp.concatenate([ours, returned], axis=1)
    return jnp.swapaxes(mine, 0, 1)


def attend_ranked(query_rows, keys, values, gate_rows):
    heads, rows, width = query_rows.shape
    scale = 1.0 / math.sqrt(width)
    ranks = jnp.arange(rows, dtype=jnp.int32)
    scores = jnp.einsum("erd,ekd->erk", query_rows, keys, preferred_element_type=jnp.float32) * scale
    visible = ranks[None, None, :] <= ranks[None, :, None]
    scores = jnp.where(visible, scores, NEGATIVE)
    leading = jnp.max(scores, axis=2, keepdims=True)
    weights = jnp.where(visible, jnp.exp(scores - leading), 0.0)
    total = jnp.sum(weights, axis=2, keepdims=True)
    mixed = (
        jnp.einsum("erk,ekd->erd", weights.astype(jnp.bfloat16), values, preferred_element_type=jnp.float32)
        / total
    )
    return (mixed * jax.nn.sigmoid(gate_rows)[:, :, None]).astype(jnp.bfloat16)


def sparse_heads(queries, keys, values, gate_logit, selection):
    tok_rows, heads, width = queries.shape
    start = lax.axis_index("seq") * tok_rows
    positions = start + jnp.arange(tok_rows, dtype=jnp.int32)
    one_hot = (selection[:, :, None] == positions[None, None, :]).astype(jnp.bfloat16)

    def pick(source):
        return jnp.einsum("ent,ted->end", one_hot, source, preferred_element_type=jnp.float32).astype(
            jnp.bfloat16
        )

    count = lax.axis_size("seq")
    local_kv = jnp.stack([pick(keys), pick(values)], axis=0)
    kinds, heads_, chosen, width_ = local_kv.shape
    pieces = local_kv.reshape(kinds, heads_, count, chosen // count, width_)
    arrived = lax.all_to_all(pieces, "seq", 2, 2, tiled=True)
    own = jnp.sum(arrived.astype(jnp.float32), axis=2).astype(jnp.bfloat16)
    picked_kv = lax.all_gather(own, "seq", axis=2, tiled=True)
    picked_q = pick(queries)
    gate_rows = jnp.einsum("ent,et->en", one_hot, gate_logit, preferred_element_type=jnp.float32)
    results = attend_ranked(picked_q, picked_kv[0], picked_kv[1], gate_rows)
    return jnp.einsum("ent,end->ted", one_hot, results, preferred_element_type=jnp.float32).astype(
        jnp.bfloat16
    )


def local(q_dense, k_dense, v_dense, q_expert, k_expert, v_expert, gate_logit, selection):
    dense_out = dense_heads(q_dense, k_dense, v_dense)
    expert_out = sparse_heads(q_expert, k_expert, v_expert, gate_logit, selection)
    return (dense_out, expert_out)


def solution(mesh):
    rows = P(("dp", "seq"), "head", None)
    placed = (rows, rows, rows, rows, rows, rows, P("head", ("dp", "seq")), P("head", "dp"))
    return jax.shard_map(
        local,
        mesh=mesh,
        in_specs=placed,
        out_specs=(rows, rows),
        check_vma=False,
    )
```

```python
import functools
import math

import jax
import jax.numpy as jnp
from jax import lax
from jax.experimental import pallas as pl
from jax.experimental.pallas import tpu as pltpu
from jax.sharding import PartitionSpec as P

NEGATIVE = -1e30
KEY_BLOCK = 2048


def flash_kernel(info_ref, q_ref, k_ref, v_ref, own_ref, lent_ref, *, scale, block):
    part = pl.program_id(1)
    last = info_ref[part]
    offset = info_ref[2 + part]
    rows_n = q_ref.shape[2]

    def update(j, carry, masked):
        m_prev, l_prev, acc = carry
        per = block // k_ref.shape[1]
        first = pl.multiple_of(j * per, per)
        keys = k_ref[pl.ds(first, per)].reshape(block, k_ref.shape[2])
        scores = lax.dot_general(
            q_ref[0, 0], keys, (((1,), (1,)), ((), ())),
            preferred_element_type=jnp.float32,
        ) * scale
        if masked:
            rows = lax.broadcasted_iota(jnp.int32, scores.shape, 0) + offset
            cols = lax.broadcasted_iota(jnp.int32, scores.shape, 1)
            scores = jnp.where(cols <= rows, scores, NEGATIVE)
        m_new = jnp.maximum(m_prev, jnp.max(scores, axis=1, keepdims=True))
        shrink = jnp.exp(m_prev - m_new)
        weights = jnp.exp(scores - m_new)
        l_new = l_prev * shrink + jnp.sum(weights, axis=1, keepdims=True)
        moved = jnp.dot(
            weights.astype(jnp.bfloat16), v_ref[pl.ds(first, per)].reshape(block, v_ref.shape[2]),
            preferred_element_type=jnp.float32,
        )
        return m_new, l_new, acc * shrink + moved

    init = (
        jnp.full((rows_n, 1), NEGATIVE, jnp.float32),
        jnp.zeros((rows_n, 1), jnp.float32),
        jnp.zeros((rows_n, q_ref.shape[3]), jnp.float32),
    )
    carry = lax.fori_loop(0, last, lambda j, c: update(j, c, False), init)
    m_f, l_f, acc_f = update(last, carry, True)
    result = (acc_f / l_f).astype(own_ref.dtype)

    @pl.when(part == 0)
    def _():
        own_ref[0] = result

    @pl.when(part == 1)
    def _():
        lent_ref[0] = result


def dense_flash(info, queries, stacked):
    parts, heads, rows, width = queries.shape
    pieces, kinds, heads_kv, sub, width_kv = stacked.shape
    length = pieces * sub
    block = KEY_BLOCK
    scale = 1.0 / math.sqrt(width)
    return pl.pallas_call(
        functools.partial(flash_kernel, scale=scale, block=block),
        out_shape=[jax.ShapeDtypeStruct((heads, rows, width), jnp.bfloat16)] * 2,
        grid_spec=pltpu.PrefetchScalarGridSpec(
            num_scalar_prefetch=1,
            grid=(heads, parts),
            in_specs=[
                pl.BlockSpec((1, 1, rows, width), lambda h, p, c: (p, h, 0, 0)),
                pl.BlockSpec((pieces, None, None, sub, width), lambda h, p, c: (0, 0, h, 0, 0)),
                pl.BlockSpec((pieces, None, None, sub, width), lambda h, p, c: (0, 1, h, 0, 0)),
            ],
            out_specs=[pl.BlockSpec((1, rows, width), lambda h, p, c: (h, 0, 0))] * 2,
        ),
        compiler_params=pltpu.CompilerParams(dimension_semantics=("arbitrary", "arbitrary")),
        cost_estimate=pl.CostEstimate(
            flops=2 * parts * heads * rows * length * width,
            transcendentals=parts * heads * rows * length // 2,
            bytes_accessed=stacked.size + 4 * queries.size,
        ),
    )(info, queries, stacked, stacked)


def dense_heads(queries, keys, values):
    tok_rows, heads, width = queries.shape
    count = lax.axis_size("seq")
    me = lax.axis_index("seq").astype(jnp.int32)
    partner = count - 1 - me
    half = tok_rows // 2
    swap = [(i, count - 1 - i) for i in range(count)]
    stacked = jnp.stack([jnp.swapaxes(keys, 0, 1), jnp.swapaxes(values, 0, 1)], axis=0)
    gathered = lax.all_gather(stacked, "seq", axis=0)
    rows_first = jnp.swapaxes(queries, 0, 1)
    lent = lax.ppermute(rows_first[:, half:], "seq", swap)
    both = jnp.stack([rows_first[:, :half], lent], axis=0)
    ends = jnp.stack([me * tok_rows, partner * tok_rows + half])
    lasts = (ends + half - 1) // KEY_BLOCK
    info = jnp.concatenate([lasts, ends - lasts * KEY_BLOCK]).astype(jnp.int32)
    ours, theirs = dense_flash(info, both, gathered)
    returned = lax.ppermute(theirs, "seq", swap)
    mine = jnp.concatenate([ours, returned], axis=1)
    return jnp.swapaxes(mine, 0, 1)


def attend_ranked(query_rows, keys, values, gate_rows):
    heads, rows, width = query_rows.shape
    scale = 1.0 / math.sqrt(width)
    ranks = jnp.arange(rows, dtype=jnp.int32)
    scores = jnp.einsum("erd,ekd->erk", query_rows, keys, preferred_element_type=jnp.float32) * scale
    visible = ranks[None, None, :] <= ranks[None, :, None]
    scores = jnp.where(visible, scores, NEGATIVE)
    leading = jnp.max(scores, axis=2, keepdims=True)
    weights = jnp.where(visible, jnp.exp(scores - leading), 0.0)
    total = jnp.sum(weights, axis=2, keepdims=True)
    mixed = (
        jnp.einsum("erk,ekd->erd", weights.astype(jnp.bfloat16), values, preferred_element_type=jnp.float32)
        / total
    )
    return (mixed * jax.nn.sigmoid(gate_rows)[:, :, None]).astype(jnp.bfloat16)


def sparse_heads(queries, keys, values, gate_logit, selection):
    tok_rows, heads, width = queries.shape
    start = lax.axis_index("seq") * tok_rows
    positions = start + jnp.arange(tok_rows, dtype=jnp.int32)
    one_hot = (selection[:, :, None] == positions[None, None, :]).astype(jnp.bfloat16)

    def pick(source):
        return jnp.einsum("ent,ted->end", one_hot, source, preferred_element_type=jnp.float32).astype(
            jnp.bfloat16
        )

    count = lax.axis_size("seq")
    local_kv = jnp.stack([pick(keys), pick(values)], axis=0)
    kinds, heads_, chosen, width_ = local_kv.shape
    pieces = local_kv.reshape(kinds, heads_, count, chosen // count, width_)
    arrived = lax.all_to_all(pieces, "seq", 2, 2, tiled=True)
    own = jnp.sum(arrived.astype(jnp.float32), axis=2).astype(jnp.bfloat16)
    me = lax.axis_index("seq")
    picked_kv = own
    step = 1
    while step < count:
        arrived_part = lax.ppermute(picked_kv, "seq", [(i, i ^ step) for i in range(count)])
        low = (me & step) == 0
        picked_kv = jnp.where(
            low,
            jnp.concatenate([picked_kv, arrived_part], axis=2),
            jnp.concatenate([arrived_part, picked_kv], axis=2),
        )
        step *= 2
    picked_q = pick(queries)
    gate_rows = jnp.einsum("ent,et->en", one_hot, gate_logit, preferred_element_type=jnp.float32)
    results = attend_ranked(picked_q, picked_kv[0], picked_kv[1], gate_rows)
    return jnp.einsum("ent,end->ted", one_hot, results, preferred_element_type=jnp.float32).astype(
        jnp.bfloat16
    )


def local(q_dense, k_dense, v_dense, q_expert, k_expert, v_expert, gate_logit, selection):
    dense_out = dense_heads(q_dense, k_dense, v_dense)
    expert_out = sparse_heads(q_expert, k_expert, v_expert, gate_logit, selection)
    return (dense_out, expert_out)


def solution(mesh):
    rows = P(("dp", "seq"), "head", None)
    placed = (rows, rows, rows, rows, rows, rows, P("head", ("dp", "seq")), P("head", "dp"))
    return jax.shard_map(
        local,
        mesh=mesh,
        in_specs=placed,
        out_specs=(rows, rows),
        check_vma=False,
    )
```

```python
import functools
import math

import jax
import jax.numpy as jnp
from jax import lax
from jax.experimental import pallas as pl
from jax.experimental.pallas import tpu as pltpu
from jax.sharding import PartitionSpec as P

NEGATIVE = -1e30
KEY_BLOCK = 2048
TAIL_BLOCK = 512


def flash_kernel(info_ref, q_ref, k_ref, v_ref, own_ref, lent_ref, *, scale, block):
    part = pl.program_id(1)
    last = info_ref[part]
    offset = info_ref[2 + part]
    rows_n = q_ref.shape[2]

    def update(j, carry, masked, wide=block):
        m_prev, l_prev, acc = carry
        first = pl.multiple_of(j * block, block)
        scores = lax.dot_general(
            q_ref[0, 0], k_ref[0, pl.ds(first, wide), :], (((1,), (1,)), ((), ())),
            preferred_element_type=jnp.float32,
        ) * scale
        if masked:
            rows = lax.broadcasted_iota(jnp.int32, scores.shape, 0) + offset
            cols = lax.broadcasted_iota(jnp.int32, scores.shape, 1)
            scores = jnp.where(cols <= rows, scores, NEGATIVE)
        m_new = jnp.maximum(m_prev, jnp.max(scores, axis=1, keepdims=True))
        shrink = jnp.exp(m_prev - m_new)
        weights = jnp.exp(scores - m_new)
        l_new = l_prev * shrink + jnp.sum(weights, axis=1, keepdims=True)
        moved = jnp.dot(
            weights.astype(jnp.bfloat16), v_ref[0, pl.ds(first, wide), :],
            preferred_element_type=jnp.float32,
        )
        return m_new, l_new, acc * shrink + moved

    init = (
        jnp.full((rows_n, 1), NEGATIVE, jnp.float32),
        jnp.zeros((rows_n, 1), jnp.float32),
        jnp.zeros((rows_n, q_ref.shape[3]), jnp.float32),
    )
    carry = lax.fori_loop(0, last, lambda j, c: update(j, c, False), init)
    widths = list(range(TAIL_BLOCK, block + 1, TAIL_BLOCK))
    which = (offset + rows_n - 1) // TAIL_BLOCK
    m_f, l_f, acc_f = lax.switch(
        which, [lambda c, w=w: update(last, c, True, w) for w in widths], carry
    )
    result = (acc_f / l_f).astype(own_ref.dtype)

    @pl.when(part == 0)
    def _():
        own_ref[0] = result

    @pl.when(part == 1)
    def _():
        lent_ref[0] = result


def dense_flash(info, queries, stacked):
    parts, heads, rows, width = queries.shape
    length = stacked.shape[2]
    block = KEY_BLOCK
    scale = 1.0 / math.sqrt(width)
    return pl.pallas_call(
        functools.partial(flash_kernel, scale=scale, block=block),
        out_shape=[jax.ShapeDtypeStruct((heads, rows, width), jnp.bfloat16)] * 2,
        grid_spec=pltpu.PrefetchScalarGridSpec(
            num_scalar_prefetch=1,
            grid=(heads, parts),
            in_specs=[
                pl.BlockSpec((1, 1, rows, width), lambda h, p, c: (p, h, 0, 0)),
                pl.BlockSpec((None, 1, length, width), lambda h, p, c: (0, h, 0, 0)),
                pl.BlockSpec((None, 1, length, width), lambda h, p, c: (1, h, 0, 0)),
            ],
            out_specs=[pl.BlockSpec((1, rows, width), lambda h, p, c: (h, 0, 0))] * 2,
        ),
        compiler_params=pltpu.CompilerParams(dimension_semantics=("arbitrary", "arbitrary")),
        cost_estimate=pl.CostEstimate(
            flops=2 * parts * heads * rows * length * width,
            transcendentals=parts * heads * rows * length // 2,
            bytes_accessed=stacked.size + 4 * queries.size,
        ),
    )(info, queries, stacked, stacked)


def dense_heads(queries, keys, values):
    tok_rows, heads, width = queries.shape
    count = lax.axis_size("seq")
    me = lax.axis_index("seq").astype(jnp.int32)
    partner = count - 1 - me
    half = tok_rows // 2
    swap = [(i, count - 1 - i) for i in range(count)]
    stacked = jnp.stack([jnp.swapaxes(keys, 0, 1), jnp.swapaxes(values, 0, 1)], axis=0)
    gathered = lax.all_gather(stacked, "seq", axis=2, tiled=True)
    rows_first = jnp.swapaxes(queries, 0, 1)
    lent = lax.ppermute(rows_first[:, half:], "seq", swap)
    both = jnp.stack([rows_first[:, :half], lent], axis=0)
    ends = jnp.stack([me * tok_rows, partner * tok_rows + half])
    lasts = (ends + half - 1) // KEY_BLOCK
    info = jnp.concatenate([lasts, ends - lasts * KEY_BLOCK]).astype(jnp.int32)
    ours, theirs = dense_flash(info, both, gathered)
    returned = lax.ppermute(theirs, "seq", swap)
    mine = jnp.concatenate([ours, returned], axis=1)
    return jnp.swapaxes(mine, 0, 1)


def attend_ranked(query_rows, keys, values, gate_rows):
    heads, rows, width = query_rows.shape
    scale = 1.0 / math.sqrt(width)
    ranks = jnp.arange(rows, dtype=jnp.int32)
    scores = jnp.einsum("erd,ekd->erk", query_rows, keys, preferred_element_type=jnp.float32) * scale
    visible = ranks[None, None, :] <= ranks[None, :, None]
    scores = jnp.where(visible, scores, NEGATIVE)
    leading = jnp.max(scores, axis=2, keepdims=True)
    weights = jnp.where(visible, jnp.exp(scores - leading), 0.0)
    total = jnp.sum(weights, axis=2, keepdims=True)
    mixed = (
        jnp.einsum("erk,ekd->erd", weights.astype(jnp.bfloat16), values, preferred_element_type=jnp.float32)
        / total
    )
    return (mixed * jax.nn.sigmoid(gate_rows)[:, :, None]).astype(jnp.bfloat16)


def sparse_heads(queries, keys, values, gate_logit, selection):
    tok_rows, heads, width = queries.shape
    start = lax.axis_index("seq") * tok_rows
    positions = start + jnp.arange(tok_rows, dtype=jnp.int32)
    one_hot = (selection[:, :, None] == positions[None, None, :]).astype(jnp.bfloat16)

    def pick(source):
        return jnp.einsum("ent,ted->end", one_hot, source, preferred_element_type=jnp.float32).astype(
            jnp.bfloat16
        )

    count = lax.axis_size("seq")
    local_kv = jnp.stack([pick(keys), pick(values)], axis=0)
    kinds, heads_, chosen, width_ = local_kv.shape
    pieces = local_kv.reshape(kinds, heads_, count, chosen // count, width_)
    arrived = lax.all_to_all(pieces, "seq", 2, 2, tiled=True)
    own = jnp.sum(arrived.astype(jnp.float32), axis=2).astype(jnp.bfloat16)
    picked_kv = lax.all_gather(own, "seq", axis=2, tiled=True)
    picked_q = pick(queries)
    gate_rows = jnp.einsum("ent,et->en", one_hot, gate_logit, preferred_element_type=jnp.float32)
    results = attend_ranked(picked_q, picked_kv[0], picked_kv[1], gate_rows)
    return jnp.einsum("ent,end->ted", one_hot, results, preferred_element_type=jnp.float32).astype(
        jnp.bfloat16
    )


def local(q_dense, k_dense, v_dense, q_expert, k_expert, v_expert, gate_logit, selection):
    dense_out = dense_heads(q_dense, k_dense, v_dense)
    expert_out = sparse_heads(q_expert, k_expert, v_expert, gate_logit, selection)
    return (dense_out, expert_out)


def solution(mesh):
    rows = P(("dp", "seq"), "head", None)
    placed = (rows, rows, rows, rows, rows, rows, P("head", ("dp", "seq")), P("head", "dp"))
    return jax.shard_map(
        local,
        mesh=mesh,
        in_specs=placed,
        out_specs=(rows, rows),
        check_vma=False,
    )
```

```python
import functools
import math

import jax
import jax.numpy as jnp
from jax import lax
from jax.experimental import pallas as pl
from jax.experimental.pallas import tpu as pltpu
from jax.sharding import PartitionSpec as P

NEGATIVE = -1e30
KEY_BLOCK = 4096
TAIL_BLOCK = 512


def flash_kernel(info_ref, q_ref, k_ref, v_ref, own_ref, lent_ref, *, scale, block):
    part = pl.program_id(1)
    last = info_ref[part]
    offset = info_ref[2 + part]
    rows_n = q_ref.shape[2]

    def update(j, carry, masked, wide=block):
        m_prev, l_prev, acc = carry
        first = pl.multiple_of(j * block, block)
        scores = lax.dot_general(
            q_ref[0, 0], k_ref[0, pl.ds(first, wide), :], (((1,), (1,)), ((), ())),
            preferred_element_type=jnp.float32,
        ) * scale
        if masked:
            rows = lax.broadcasted_iota(jnp.int32, scores.shape, 0) + offset
            cols = lax.broadcasted_iota(jnp.int32, scores.shape, 1)
            scores = jnp.where(cols <= rows, scores, NEGATIVE)
        m_new = jnp.maximum(m_prev, jnp.max(scores, axis=1, keepdims=True))
        shrink = jnp.exp(m_prev - m_new)
        weights = jnp.exp(scores - m_new)
        l_new = l_prev * shrink + jnp.sum(weights, axis=1, keepdims=True)
        moved = jnp.dot(
            weights.astype(jnp.bfloat16), v_ref[0, pl.ds(first, wide), :],
            preferred_element_type=jnp.float32,
        )
        return m_new, l_new, acc * shrink + moved

    init = (
        jnp.full((rows_n, 1), NEGATIVE, jnp.float32),
        jnp.zeros((rows_n, 1), jnp.float32),
        jnp.zeros((rows_n, q_ref.shape[3]), jnp.float32),
    )
    carry = lax.fori_loop(0, last, lambda j, c: update(j, c, False), init)
    widths = list(range(TAIL_BLOCK, block + 1, TAIL_BLOCK))
    which = (offset + rows_n - 1) // TAIL_BLOCK
    m_f, l_f, acc_f = lax.switch(
        which, [lambda c, w=w: update(last, c, True, w) for w in widths], carry
    )
    result = (acc_f / l_f).astype(own_ref.dtype)

    @pl.when(part == 0)
    def _():
        own_ref[0] = result

    @pl.when(part == 1)
    def _():
        lent_ref[0] = result


def dense_flash(info, queries, stacked):
    parts, heads, rows, width = queries.shape
    length = stacked.shape[2]
    block = KEY_BLOCK
    scale = 1.0 / math.sqrt(width)
    return pl.pallas_call(
        functools.partial(flash_kernel, scale=scale, block=block),
        out_shape=[jax.ShapeDtypeStruct((heads, rows, width), jnp.bfloat16)] * 2,
        grid_spec=pltpu.PrefetchScalarGridSpec(
            num_scalar_prefetch=1,
            grid=(heads, parts),
            in_specs=[
                pl.BlockSpec((1, 1, rows, width), lambda h, p, c: (p, h, 0, 0)),
                pl.BlockSpec((None, 1, length, width), lambda h, p, c: (0, h, 0, 0)),
                pl.BlockSpec((None, 1, length, width), lambda h, p, c: (1, h, 0, 0)),
            ],
            out_specs=[pl.BlockSpec((1, rows, width), lambda h, p, c: (h, 0, 0))] * 2,
        ),
        compiler_params=pltpu.CompilerParams(dimension_semantics=("arbitrary", "arbitrary")),
        cost_estimate=pl.CostEstimate(
            flops=2 * parts * heads * rows * length * width,
            transcendentals=parts * heads * rows * length // 2,
            bytes_accessed=stacked.size + 4 * queries.size,
        ),
    )(info, queries, stacked, stacked)


def dense_heads(queries, keys, values):
    tok_rows, heads, width = queries.shape
    count = lax.axis_size("seq")
    me = lax.axis_index("seq").astype(jnp.int32)
    partner = count - 1 - me
    half = tok_rows // 2
    swap = [(i, count - 1 - i) for i in range(count)]
    stacked = jnp.stack([jnp.swapaxes(keys, 0, 1), jnp.swapaxes(values, 0, 1)], axis=0)
    gathered = lax.all_gather(stacked, "seq", axis=2, tiled=True)
    rows_first = jnp.swapaxes(queries, 0, 1)
    lent = lax.ppermute(rows_first[:, half:], "seq", swap)
    both = jnp.stack([rows_first[:, :half], lent], axis=0)
    ends = jnp.stack([me * tok_rows, partner * tok_rows + half])
    lasts = (ends + half - 1) // KEY_BLOCK
    info = jnp.concatenate([lasts, ends - lasts * KEY_BLOCK]).astype(jnp.int32)
    ours, theirs = dense_flash(info, both, gathered)
    returned = lax.ppermute(theirs, "seq", swap)
    mine = jnp.concatenate([ours, returned], axis=1)
    return jnp.swapaxes(mine, 0, 1)


def attend_ranked(query_rows, keys, values, gate_rows):
    heads, rows, width = query_rows.shape
    scale = 1.0 / math.sqrt(width)
    ranks = jnp.arange(rows, dtype=jnp.int32)
    scores = jnp.einsum("erd,ekd->erk", query_rows, keys, preferred_element_type=jnp.float32) * scale
    visible = ranks[None, None, :] <= ranks[None, :, None]
    scores = jnp.where(visible, scores, NEGATIVE)
    leading = jnp.max(scores, axis=2, keepdims=True)
    weights = jnp.where(visible, jnp.exp(scores - leading), 0.0)
    total = jnp.sum(weights, axis=2, keepdims=True)
    mixed = (
        jnp.einsum("erk,ekd->erd", weights.astype(jnp.bfloat16), values, preferred_element_type=jnp.float32)
        / total
    )
    return (mixed * jax.nn.sigmoid(gate_rows)[:, :, None]).astype(jnp.bfloat16)


def sparse_heads(queries, keys, values, gate_logit, selection):
    tok_rows, heads, width = queries.shape
    start = lax.axis_index("seq") * tok_rows
    positions = start + jnp.arange(tok_rows, dtype=jnp.int32)
    one_hot = (selection[:, :, None] == positions[None, None, :]).astype(jnp.bfloat16)

    def pick(source):
        return jnp.einsum("ent,ted->end", one_hot, source, preferred_element_type=jnp.float32).astype(
            jnp.bfloat16
        )

    count = lax.axis_size("seq")
    local_kv = jnp.stack([pick(keys), pick(values)], axis=0)
    kinds, heads_, chosen, width_ = local_kv.shape
    pieces = local_kv.reshape(kinds, heads_, count, chosen // count, width_)
    arrived = lax.all_to_all(pieces, "seq", 2, 2, tiled=True)
    own = jnp.sum(arrived.astype(jnp.float32), axis=2).astype(jnp.bfloat16)
    picked_kv = lax.all_gather(own, "seq", axis=2, tiled=True)
    picked_q = pick(queries)
    gate_rows = jnp.einsum("ent,et->en", one_hot, gate_logit, preferred_element_type=jnp.float32)
    results = attend_ranked(picked_q, picked_kv[0], picked_kv[1], gate_rows)
    return jnp.einsum("ent,end->ted", one_hot, results, preferred_element_type=jnp.float32).astype(
        jnp.bfloat16
    )


def local(q_dense, k_dense, v_dense, q_expert, k_expert, v_expert, gate_logit, selection):
    dense_out = dense_heads(q_dense, k_dense, v_dense)
    expert_out = sparse_heads(q_expert, k_expert, v_expert, gate_logit, selection)
    return (dense_out, expert_out)


def solution(mesh):
    rows = P(("dp", "seq"), "head", None)
    placed = (rows, rows, rows, rows, rows, rows, P("head", ("dp", "seq")), P("head", "dp"))
    return jax.shard_map(
        local,
        mesh=mesh,
        in_specs=placed,
        out_specs=(rows, rows),
        check_vma=False,
    )
```

```python
import functools
import math

import jax
import jax.numpy as jnp
from jax import lax
from jax.experimental import pallas as pl
from jax.experimental.pallas import tpu as pltpu
from jax.sharding import PartitionSpec as P

NEGATIVE = -1e30
KEY_BLOCK = 4096
TAIL_BLOCK = 512
LOG2E = 1.4426950408889634


def flash_kernel(info_ref, q_ref, k_ref, v_ref, own_ref, lent_ref, *, scale, block):
    part = pl.program_id(1)
    last = info_ref[part]
    offset = info_ref[2 + part]
    rows_n = q_ref.shape[2]

    def update(j, carry, masked, wide=block):
        m_prev, l_prev, acc = carry
        first = pl.multiple_of(j * block, block)
        scores = lax.dot_general(
            q_ref[0, 0], k_ref[0, pl.ds(first, wide), :], (((1,), (1,)), ((), ())),
            preferred_element_type=jnp.float32,
        ) * (scale * LOG2E)
        if masked:
            rows = lax.broadcasted_iota(jnp.int32, scores.shape, 0) + offset
            cols = lax.broadcasted_iota(jnp.int32, scores.shape, 1)
            scores = jnp.where(cols <= rows, scores, NEGATIVE)
        m_new = jnp.maximum(m_prev, jnp.max(scores, axis=1, keepdims=True))
        shrink = jnp.exp2(m_prev - m_new)
        weights = jnp.exp2(scores - m_new)
        l_new = l_prev * shrink + jnp.sum(weights, axis=1, keepdims=True)
        moved = jnp.dot(
            weights.astype(jnp.bfloat16), v_ref[0, pl.ds(first, wide), :],
            preferred_element_type=jnp.float32,
        )
        return m_new, l_new, acc * shrink + moved

    init = (
        jnp.full((rows_n, 1), NEGATIVE, jnp.float32),
        jnp.zeros((rows_n, 1), jnp.float32),
        jnp.zeros((rows_n, q_ref.shape[3]), jnp.float32),
    )
    carry = lax.fori_loop(0, last, lambda j, c: update(j, c, False), init)
    widths = list(range(TAIL_BLOCK, block + 1, TAIL_BLOCK))
    which = (offset + rows_n - 1) // TAIL_BLOCK
    m_f, l_f, acc_f = lax.switch(
        which, [lambda c, w=w: update(last, c, True, w) for w in widths], carry
    )
    result = (acc_f / l_f).astype(own_ref.dtype)

    @pl.when(part == 0)
    def _():
        own_ref[0] = result

    @pl.when(part == 1)
    def _():
        lent_ref[0] = result


def dense_flash(info, queries, stacked):
    parts, heads, rows, width = queries.shape
    length = stacked.shape[2]
    block = KEY_BLOCK
    scale = 1.0 / math.sqrt(width)
    return pl.pallas_call(
        functools.partial(flash_kernel, scale=scale, block=block),
        out_shape=[jax.ShapeDtypeStruct((heads, rows, width), jnp.bfloat16)] * 2,
        grid_spec=pltpu.PrefetchScalarGridSpec(
            num_scalar_prefetch=1,
            grid=(heads, parts),
            in_specs=[
                pl.BlockSpec((1, 1, rows, width), lambda h, p, c: (p, h, 0, 0)),
                pl.BlockSpec((None, 1, length, width), lambda h, p, c: (0, h, 0, 0)),
                pl.BlockSpec((None, 1, length, width), lambda h, p, c: (1, h, 0, 0)),
            ],
            out_specs=[pl.BlockSpec((1, rows, width), lambda h, p, c: (h, 0, 0))] * 2,
        ),
        compiler_params=pltpu.CompilerParams(dimension_semantics=("arbitrary", "arbitrary")),
        cost_estimate=pl.CostEstimate(
            flops=2 * parts * heads * rows * length * width,
            transcendentals=parts * heads * rows * length // 2,
            bytes_accessed=stacked.size + 4 * queries.size,
        ),
    )(info, queries, stacked, stacked)


def dense_heads(queries, keys, values):
    tok_rows, heads, width = queries.shape
    count = lax.axis_size("seq")
    me = lax.axis_index("seq").astype(jnp.int32)
    partner = count - 1 - me
    half = tok_rows // 2
    swap = [(i, count - 1 - i) for i in range(count)]
    stacked = jnp.stack([jnp.swapaxes(keys, 0, 1), jnp.swapaxes(values, 0, 1)], axis=0)
    gathered = lax.all_gather(stacked, "seq", axis=2, tiled=True)
    rows_first = jnp.swapaxes(queries, 0, 1)
    lent = lax.ppermute(rows_first[:, half:], "seq", swap)
    both = jnp.stack([rows_first[:, :half], lent], axis=0)
    ends = jnp.stack([me * tok_rows, partner * tok_rows + half])
    lasts = (ends + half - 1) // KEY_BLOCK
    info = jnp.concatenate([lasts, ends - lasts * KEY_BLOCK]).astype(jnp.int32)
    ours, theirs = dense_flash(info, both, gathered)
    returned = lax.ppermute(theirs, "seq", swap)
    mine = jnp.concatenate([ours, returned], axis=1)
    return jnp.swapaxes(mine, 0, 1)


def attend_ranked(query_rows, keys, values, gate_rows):
    heads, rows, width = query_rows.shape
    scale = 1.0 / math.sqrt(width)
    ranks = jnp.arange(rows, dtype=jnp.int32)
    scores = jnp.einsum("erd,ekd->erk", query_rows, keys, preferred_element_type=jnp.float32) * scale
    visible = ranks[None, None, :] <= ranks[None, :, None]
    scores = jnp.where(visible, scores, NEGATIVE)
    leading = jnp.max(scores, axis=2, keepdims=True)
    weights = jnp.where(visible, jnp.exp(scores - leading), 0.0)
    total = jnp.sum(weights, axis=2, keepdims=True)
    mixed = (
        jnp.einsum("erk,ekd->erd", weights.astype(jnp.bfloat16), values, preferred_element_type=jnp.float32)
        / total
    )
    return (mixed * jax.nn.sigmoid(gate_rows)[:, :, None]).astype(jnp.bfloat16)


def sparse_heads(queries, keys, values, gate_logit, selection):
    tok_rows, heads, width = queries.shape
    start = lax.axis_index("seq") * tok_rows
    positions = start + jnp.arange(tok_rows, dtype=jnp.int32)
    one_hot = (selection[:, :, None] == positions[None, None, :]).astype(jnp.bfloat16)

    def pick(source):
        return jnp.einsum("ent,ted->end", one_hot, source, preferred_element_type=jnp.float32).astype(
            jnp.bfloat16
        )

    count = lax.axis_size("seq")
    local_kv = jnp.stack([pick(keys), pick(values)], axis=0)
    kinds, heads_, chosen, width_ = local_kv.shape
    pieces = local_kv.reshape(kinds, heads_, count, chosen // count, width_)
    arrived = lax.all_to_all(pieces, "seq", 2, 2, tiled=True)
    own = jnp.sum(arrived.astype(jnp.float32), axis=2).astype(jnp.bfloat16)
    picked_kv = lax.all_gather(own, "seq", axis=2, tiled=True)
    picked_q = pick(queries)
    gate_rows = jnp.einsum("ent,et->en", one_hot, gate_logit, preferred_element_type=jnp.float32)
    results = attend_ranked(picked_q, picked_kv[0], picked_kv[1], gate_rows)
    return jnp.einsum("ent,end->ted", one_hot, results, preferred_element_type=jnp.float32).astype(
        jnp.bfloat16
    )


def local(q_dense, k_dense, v_dense, q_expert, k_expert, v_expert, gate_logit, selection):
    dense_out = dense_heads(q_dense, k_dense, v_dense)
    expert_out = sparse_heads(q_expert, k_expert, v_expert, gate_logit, selection)
    return (dense_out, expert_out)


def solution(mesh):
    rows = P(("dp", "seq"), "head", None)
    placed = (rows, rows, rows, rows, rows, rows, P("head", ("dp", "seq")), P("head", "dp"))
    return jax.shard_map(
        local,
        mesh=mesh,
        in_specs=placed,
        out_specs=(rows, rows),
        check_vma=False,
    )
```
